128 devices in a mesh: dp: 32 (over y, x, core), mp: 4 (over z).
Axes of the slice: x: 4, y: 4, z: 4, core: 2. Of those that a mesh axis runs over, the one named last changes fastest.
Arguments:
- hidden: bfloat16 [4096, 2560], P('dp', 'mp'), may hold values from -6 to 6
- norm_gain: bfloat16 [2560], replicated, may hold values from 0.5 to 1.5
- shared_gate: bfloat16 [2560, 3072], P(None, 'mp'), may hold values from -0.125 to 0.125
- shared_up: bfloat16 [2560, 3072], P(None, 'mp'), may hold values from -0.125 to 0.125
- shared_down: bfloat16 [3072, 2560], P('mp'), may hold values from -0.109375 to 0.109375
- expert_gate: bfloat16 [64, 2560, 1536], P('dp', None, 'mp'), may hold values from -0.125 to 0.125
- expert_up: bfloat16 [64, 2560, 1536], P('dp', None, 'mp'), may hold values from -0.125 to 0.125
- expert_down: bfloat16 [64, 1536, 2560], P('dp', 'mp'), may hold values from -0.15625 to 0.15625
- adapter_in: bfloat16 [64, 3072, 16], P('dp', 'mp'), may hold values from -0.109375 to 0.109375
- adapter_out: bfloat16 [64, 16, 2560], P('dp'), may hold values from -1.5 to 1.5
- active: int32 [16], replicated, may hold values from 0 to 63, as said below
- lengths: int32 [64], replicated, may hold values from 1 to 1024, 4096 in all
- request_adapter: int32 [64], replicated, may hold values from 0 to 15
- routes: int32 [4096, 6], P('dp'), may hold values from 0 to 63, all different within a row; in each aligned block of 128 rows (0 to 127, 128 to 255, ...) at most 16 rows name the same one
- route_weights: float32 [4096, 6], P('dp'), may hold values from 0.05 to 0.35
Outputs:
- layer_out: bfloat16 [4096, 2560], P('dp', 'mp')
The draws below stay inside these ranges and needn't reach their ends.
Inputs may be any that keep to these rules, and one draw needn't show every extreme that they name: `active`: the entries are distinct. `routes`: within the 128 rows of one index of dp no expert is named more than 16 times, and that many is reached; a row names distinct experts.
All inputs are finite; a program needn't handle non-finite values.
Results may differ from the reference program's by a relative error of at most 0.015.
Values may be sent and summed in bfloat16 or wider, within the bound.
No kernel may reach another device: no remote copies, remote signals or barrier semaphores. Data moves between devices by JAX's collectives and lax.ppermute only.
A program may use at most 128 MiB of HBM per device.

```python
import math
import jax
import jax.numpy as jnp
import numpy as np
from jax import lax

D = 2560
FF = 1536
SFF = 3072
EXPERTS = 64
TOPK = 6
ADAPTERS = 64
ACTIVE = 16
RANK = 16
TOK_DEV = 128
REQUESTS = 64
TOKENS = 4096
LONGEST = 1024
CAP = 16
N_DP = 32


def draw_active(key, part):
    shuffled = jax.random.permutation(key, ADAPTERS)
    return shuffled[:ACTIVE].astype(jnp.int32)


def touch_ends(values, rng, low, largest):
    index_at = [jax.random.randint(jax.random.fold_in(rng, axis), (), 0, length) for axis, length in enumerate(values.shape)]
    main_axis = values.shape.index(max(values.shape))
    beside = index_at[:main_axis] + [(index_at[main_axis] + 1) % values.shape[main_axis]] + index_at[main_axis + 1:]
    return values.at[tuple(index_at)].set(low).at[tuple(beside)].set(largest)


def block_levels(own_key, shape, split, low, largest):
    gain, own = 1.0, jax.random.fold_in(own_key, 6)
    for position, blocks in split:
        heights = jnp.exp(jax.random.uniform(jax.random.fold_in(own, position), (blocks,), jnp.float32, low / len(split), largest / len(split)))
        gain = gain * jnp.repeat(heights, shape[position] // blocks).reshape([-1 if axis == position else 1 for axis in range(len(shape))])
    return gain


def profile(number_of, total, limit, skew):
    loads = [(1 << 20) // math.isqrt(rank ** skew) + 1 for rank in range(2, number_of + 1)]
    spare, counts = total - limit - (number_of - 1), [1] * (number_of - 1)
    while spare > 0:
        free = [i for i in range(number_of - 1) if counts[i] < limit]
        mass, budget = sum([loads[i] for i in free]), spare
        for i in free:
            more = min(limit - counts[i], max(1, budget * loads[i] // mass), spare)
            counts[i] = counts[i] + more
            spare = spare - more
    return np.array([limit] + counts)


def uneven_parts(key, amount, total, most, skew):
    if amount == 2:
        one = jax.random.randint(key, (), max(1, total - most), min(most, total - 1) + 1)
        return jnp.stack([one, total - one])
    tallies = jnp.asarray(profile(amount, total, most, skew), jnp.int32)
    twos = (amount - 1) // 2
    giver, taker = tallies[1:1 + 2 * twos:2], tallies[2:2 + 2 * twos:2]
    slack = jnp.minimum(giver - 1, most - taker)
    moved = jax.random.randint(jax.random.fold_in(key, 1), (twos,), 0, 1 << 20) % (slack + 1)
    tallies = tallies.at[1:1 + 2 * twos:2].set(giver - moved).at[2:2 + 2 * twos:2].set(taker + moved)
    return tallies[jax.random.permutation(jax.random.fold_in(key, 2), amount)]


def routed_block(own_key, own, number, rows, number_of, top, most, lean):
    ranking = jax.random.permutation(own_key, number_of)
    crowded, ordinary = load_shares(number_of, rows * top, most, lean, True), load_shares(number_of, rows * top, most, lean, False)
    places = jnp.arange(number_of)

    def named(sizes, turn):
        used = int((sizes > 0).sum())
        fixed = max(1, used // 4)
        moved = fixed + (places - fixed + turn * (used - fixed)) % max(1, number_of - fixed)
        return jnp.zeros((number_of,), jnp.int32).at[ranking[jnp.where(places < fixed, places, moved)]].set(jnp.asarray(sizes, jnp.int32))

    sizes = jnp.where(number % 4 == 0, named(crowded, number // 4), named(ordinary, number - number // 4 - 1))
    mixed = jax.random.permutation(jax.random.fold_in(own, 3), number_of)
    donor, taker = mixed[0:number_of // 2 * 2:2], mixed[1:number_of // 2 * 2:2]
    margin = jnp.minimum(sizes[donor] - 1, most - sizes[taker]) // 2
    margin = jnp.where((donor == ranking[0]) | (taker == ranking[0]) | (sizes[taker] == 0), 0, jnp.maximum(margin, 0))
    moved = jax.random.randint(jax.random.fold_in(own, 4), (number_of // 2,), 0, 1 << 20) % (margin + 1)
    sizes = sizes.at[donor].add(-moved).at[taker].add(moved)
    labels = jnp.searchsorted(jnp.cumsum(sizes), jnp.arange(rows * top), side="right").astype(jnp.int32)
    grid = labels.reshape(top, rows).T
    grid = grid[jax.random.permutation(jax.random.fold_in(own, 1), rows)]
    turn = jax.random.randint(jax.random.fold_in(own, 2), (rows, 1), 0, top)
    return jnp.take_along_axis(grid, (jnp.arange(top)[None, :] + turn) % top, axis=1)


def load_shares(count, total, limit, slope, full):
    portions = [(1 << 20) // math.isqrt(standing ** slope) + 1 for standing in range(1, count + 1)]
    largest = limit if full else min(limit, max(-(-total // count), total * portions[0] // sum(portions)))
    least = 1 if total - largest >= count - 1 else 0
    holding, surplus = [largest] + [least] * (count - 1), total - largest - least * (count - 1)
    while surplus > 0:
        movable = [i for i in range(1, count) if holding[i] < largest] or [i for i in range(1, count) if holding[i] < limit]
        pool, left = sum([portions[i] for i in movable]), surplus
        for i in movable:
            more = min(limit - holding[i], max(1, left * portions[i] // pool), surplus)
            holding[i] = holding[i] + more
            surplus = surplus - more
    return np.array(holding)


def scatter_about(rng, shape, scale, reach, pieces=(), kind=jnp.bfloat16):
    drawn = scale * jax.random.normal(rng, shape, jnp.float32)
    if pieces:
        drawn = drawn * block_levels(rng, shape, pieces, -0.22, 0.18)
    return jnp.clip(drawn, -reach, reach).astype(kind)


def setup_inputs(seed: int = 0) -> dict:
    key_list = jax.random.split(jax.random.key(seed), 16)
    hidden = scatter_about(key_list[0], (TOKENS, D), 1.0, 6.0, ((0, 32), (1, 4)))
    norm_gain = jnp.clip(1.0 + 0.1 * jax.random.normal(key_list[1], (D,), jnp.float32), 0.5, 1.5).astype(jnp.bfloat16)
    shared_gate = scatter_about(key_list[2], (D, SFF), D ** -0.5, 0.125, ((1, 4),))
    shared_up = scatter_about(key_list[3], (D, SFF), D ** -0.5, 0.125, ((1, 4),))
    shared_down = scatter_about(key_list[4], (SFF, D), SFF ** -0.5, 0.109375, ((0, 4),))
    expert_gate = scatter_about(key_list[5], (EXPERTS, D, FF), D ** -0.5, 0.125, ((0, 32), (2, 4)))
    expert_up = scatter_about(key_list[6], (EXPERTS, D, FF), D ** -0.5, 0.125, ((0, 32), (2, 4)))
    expert_down = scatter_about(key_list[7], (EXPERTS, FF, D), FF ** -0.5, 0.15625, ((0, 32), (1, 4)))
    adapter_in = scatter_about(key_list[8], (ADAPTERS, SFF, RANK), SFF ** -0.5, 0.109375, ((0, 32), (1, 4)))
    adapter_out = scatter_about(key_list[9], (ADAPTERS, RANK, D), RANK ** -0.5, 1.5, ((0, 32),))
    active = draw_active(jax.random.fold_in(key_list[15], 71), 0)
    lengths = uneven_parts(key_list[11], REQUESTS, TOKENS, LONGEST, 2).astype(jnp.int32)
    request_adapter = touch_ends(jax.random.randint(key_list[12], (REQUESTS,), 0, ACTIVE), jax.random.fold_in(key_list[12], 1), 0, ACTIVE - 1).astype(jnp.int32)
    routes_keys = jax.random.split(jax.random.fold_in(key_list[13], 1), TOKENS // TOK_DEV)
    routes_turns = jax.random.permutation(jax.random.fold_in(key_list[13], 3), TOKENS // TOK_DEV)
    routes = jax.vmap(lambda own, number: routed_block(jax.random.fold_in(key_list[13], 2), own, number, TOK_DEV, EXPERTS, TOPK, CAP, 1))(routes_keys, routes_turns).reshape((TOKENS, TOPK))
    route_weights = jnp.clip(0.05 + 0.29999999 * jax.random.uniform(key_list[14], (TOKENS, TOPK), jnp.float32) ** block_levels(key_list[14], (TOKENS, TOPK), ((0, 32),), -0.2, 0.2), 0.05, 0.35)
    return dict(hidden=hidden, norm_gain=norm_gain, shared_gate=shared_gate, shared_up=shared_up, shared_down=shared_down, expert_gate=expert_gate, expert_up=expert_up, expert_down=expert_down, adapter_in=adapter_in, adapter_out=adapter_out, active=active, lengths=lengths, request_adapter=request_adapter, routes=routes, route_weights=route_weights)


def rms_norm(hidden, norm_gain):
    values = hidden.astype(jnp.float32)
    factor = lax.rsqrt(lax.optimization_barrier(jnp.mean(values * values, axis=-1, keepdims=True)) + 1e-06)
    return (values * factor * norm_gain.astype(jnp.float32)).astype(jnp.bfloat16)

def reference(hidden, norm_gain, shared_gate, shared_up, shared_down, expert_gate, expert_up, expert_down, adapter_in, adapter_out, active, lengths, request_adapter, routes, route_weights):
    normed = rms_norm(hidden, norm_gain)
    shared_lin = jnp.dot(normed, shared_gate, preferred_element_type=jnp.float32)
    shared_pre = jnp.dot(normed, shared_up, preferred_element_type=jnp.float32)
    shared_act = (jax.nn.silu(shared_lin) * shared_pre).astype(jnp.bfloat16)
    request_end = jnp.cumsum(lengths).astype(jnp.int32)
    positions = jnp.arange(TOKENS, dtype=jnp.int32)
    request_of = lax.optimization_barrier(jnp.sum((request_end[None, :] <= positions[:, None]).astype(jnp.int32), axis=1))
    slot_of = request_adapter[request_of]
    chosen = (slot_of[:, None] == jnp.arange(ACTIVE, dtype=jnp.int32)[None, :]).astype(jnp.float32)
    in_matrix = jnp.transpose(adapter_in[active], (1, 0, 2)).reshape(SFF, ACTIVE * RANK)
    lowrank = jnp.dot(shared_act, in_matrix, preferred_element_type=jnp.float32)
    lowrank = (lowrank.reshape(TOKENS, ACTIVE, RANK) * chosen[:, :, None]).reshape(TOKENS, ACTIVE * RANK)
    out_matrix = adapter_out[active].reshape(ACTIVE * RANK, D).astype(jnp.float32)
    adapted = jnp.dot(lowrank, out_matrix, precision=lax.Precision.HIGHEST)
    shared_out = jnp.dot(shared_act, shared_down, preferred_element_type=jnp.float32) + adapted
    flat_routes = routes.reshape(-1)
    flat_weights = jnp.concatenate([route_weights.reshape(-1), jnp.zeros((1,), jnp.float32)])
    padded = jnp.concatenate([normed, jnp.zeros((1, D), normed.dtype)], axis=0)
    slot_count = N_DP * CAP

    def expert_step(total, layer):
        gate_weight, up_weight, down_weight, expert_id = layer
        hits = jnp.nonzero(flat_routes == expert_id, size=slot_count, fill_value=TOKENS * TOPK)[0].astype(jnp.int32)
        token_ids = hits // TOPK
        rows_in = padded[token_ids]
        gate_val = jnp.dot(rows_in, gate_weight, preferred_element_type=jnp.float32)
        up_val = jnp.dot(rows_in, up_weight, preferred_element_type=jnp.float32)
        inner = (jax.nn.silu(gate_val) * up_val).astype(jnp.bfloat16)
        result = jnp.dot(inner, down_weight, preferred_element_type=jnp.float32)
        total = total.at[token_ids].add(flat_weights[hits][:, None] * result)
        return (total, None)
    routed, _ = lax.scan(expert_step, jnp.zeros((TOKENS + 1, D), jnp.float32), (expert_gate, expert_up, expert_down, jnp.arange(EXPERTS, dtype=jnp.int32)))
    return (shared_out + routed[:TOKENS]).astype(jnp.bfloat16)
```

```python
import jax
import jax.numpy as jnp
from jax import lax
from jax.sharding import PartitionSpec as P


def experts_apply(slots_in, expert_gate, expert_up, expert_down):
    gate_val = jnp.einsum(
        "sjcd,jdf->sjcf", slots_in, expert_gate, preferred_element_type=jnp.float32
    )
    up_val = jnp.einsum("sjcd,jdf->sjcf", slots_in, expert_up, preferred_element_type=jnp.float32)
    inner = (jax.nn.silu(gate_val) * up_val).astype(jnp.bfloat16)
    return jnp.einsum("sjcf,jfd->sjcd", inner, expert_down, preferred_element_type=jnp.float32)


def body(
    hidden,
    norm_gain,
    shared_gate,
    shared_up,
    shared_down,
    expert_gate,
    expert_up,
    expert_down,
    adapter_in,
    adapter_out,
    active,
    lengths,
    request_adapter,
    routes,
    route_weights,
):
    tok_rows = routes.shape[0]
    top_count = routes.shape[1]
    dp_count = lax.axis_size("dp")
    mp_count = lax.axis_size("mp")
    dp_index = lax.axis_index("dp")
    mp_index = lax.axis_index("mp")
    local_experts = expert_gate.shape[0]
    total_experts = local_experts * dp_count
    capacity = mp_count * max(1, tok_rows * top_count * 4 // (total_experts * mp_count * 3))
    col_width = hidden.shape[1]
    col_start = mp_index * col_width

    active_count = active.shape[0]
    rank_width = adapter_in.shape[2]
    local_adapters = adapter_in.shape[0]
    owned_ids = dp_index * local_adapters + jnp.arange(local_adapters, dtype=jnp.int32)
    selector = (active[:, None] == owned_ids[None, :]).astype(jnp.bfloat16)
    out_cols = lax.dynamic_slice_in_dim(adapter_out, col_start, col_width, axis=2)
    picked_in = jnp.einsum(
        "ji,isr->jsr", selector, adapter_in, preferred_element_type=jnp.float32
    ).astype(jnp.bfloat16)
    picked_out = jnp.einsum(
        "ji,ird->jrd", selector, out_cols, preferred_element_type=jnp.float32
    ).astype(jnp.bfloat16)
    picked_in, picked_out = lax.psum((picked_in, picked_out), "dp")

    gathered = lax.all_gather(hidden, "mp", axis=1, tiled=True)
    values = gathered.astype(jnp.float32)
    factor = lax.rsqrt(jnp.mean(values * values, axis=-1, keepdims=True) + 1e-06)
    normed = (values * factor * norm_gain.astype(jnp.float32)).astype(jnp.bfloat16)
    width = normed.shape[1]
    shared_lin = jnp.dot(normed, shared_gate, preferred_element_type=jnp.float32)
    shared_pre = jnp.dot(normed, shared_up, preferred_element_type=jnp.float32)
    shared_act = (jax.nn.silu(shared_lin) * shared_pre).astype(jnp.bfloat16)

    request_end = jnp.cumsum(lengths)
    positions = dp_index * tok_rows + jnp.arange(tok_rows, dtype=jnp.int32)
    request_of = jnp.sum((request_end[None, :] <= positions[:, None]).astype(jnp.int32), axis=1)
    request_hot = (
        request_of[:, None] == jnp.arange(lengths.shape[0], dtype=jnp.int32)[None, :]
    ).astype(jnp.int32)
    slot_of = jnp.sum(request_hot * request_adapter[None, :], axis=1)
    chosen = (slot_of[:, None] == jnp.arange(active_count, dtype=jnp.int32)[None, :]).astype(
        jnp.float32
    )
    in_matrix = jnp.transpose(picked_in, (1, 0, 2)).reshape(
        shared_act.shape[1], active_count * rank_width
    )
    lowrank = jnp.dot(shared_act, in_matrix, preferred_element_type=jnp.float32)
    lowrank_sel = jnp.sum(lowrank.reshape(tok_rows, active_count, rank_width) * chosen[:, :, None], axis=1)
    lowrank_sel = lax.psum(lowrank_sel, "mp")
    lowrank = (chosen[:, :, None] * lowrank_sel[:, None, :]).reshape(
        tok_rows, active_count * rank_width
    )
    adapted = jnp.dot(
        lowrank,
        picked_out.reshape(active_count * rank_width, col_width).astype(jnp.float32),
        precision=lax.Precision.HIGHEST,
    )

    flat_routes = routes.reshape(-1)
    expert_hot = (
        flat_routes[:, None] == jnp.arange(total_experts, dtype=jnp.int32)[None, :]
    ).astype(jnp.int32)
    earlier = jnp.cumsum(expert_hot, axis=0) - expert_hot
    position = jnp.sum(earlier * expert_hot, axis=1)
    slot_index = (flat_routes * capacity + position).reshape(tok_rows, top_count)
    slot_count = total_experts * capacity
    slot_hit = slot_index[:, :, None] == jnp.arange(slot_count, dtype=jnp.int32)[None, None, :]
    dispatch = jnp.any(slot_hit, axis=1).astype(jnp.bfloat16)
    send_rows = jnp.einsum(
        "ts,td->sd", dispatch, normed, preferred_element_type=jnp.float32
    ).astype(jnp.bfloat16)
    send_rows = send_rows.reshape(dp_count, local_experts, capacity, width)
    returned = lax.all_to_all(
        experts_apply(
            lax.all_to_all(send_rows, "dp", split_axis=0, concat_axis=0, tiled=True),
            expert_gate,
            expert_up,
            expert_down,
        ).astype(jnp.bfloat16),
        "dp",
        split_axis=0,
        concat_axis=0,
        tiled=True,
    )
    returned = returned.reshape(slot_count, width)
    combine = jnp.sum(
        jnp.where(slot_hit, route_weights[:, :, None], 0.0), axis=1
    )
    combine_hi = combine.astype(jnp.bfloat16)
    combine_lo = (combine - combine_hi.astype(jnp.float32)).astype(jnp.bfloat16)
    routed = jnp.dot(combine_hi, returned, preferred_element_type=jnp.float32) + jnp.dot(
        combine_lo, returned, preferred_element_type=jnp.float32
    )

    partial_out = jnp.dot(shared_act, shared_down, preferred_element_type=jnp.float32) + routed
    own_cols = lax.dynamic_slice_in_dim(partial_out, col_start, col_width, axis=1) + adapted
    partial_out = lax.dynamic_update_slice_in_dim(partial_out, own_cols, col_start, axis=1)
    return lax.psum_scatter(partial_out.astype(jnp.bfloat16), "mp", scatter_dimension=1, tiled=True)


def solution(mesh):
    in_specs = (
        P("dp", "mp"),
        P(),
        P(None, "mp"),
        P(None, "mp"),
        P("mp", None),
        P("dp", None, "mp"),
        P("dp", None, "mp"),
        P("dp", "mp", None),
        P("dp", "mp", None),
        P("dp", None, None),
        P(),
        P(),
        P(),
        P("dp", None),
        P("dp", None),
    )
    out_specs = P("dp", "mp")
    return jax.shard_map(body, mesh=mesh, in_specs=in_specs, out_specs=out_specs, check_vma=False)
```

```python
import jax
import jax.numpy as jnp
from jax import lax
from jax.sharding import PartitionSpec as P


def experts_apply(slots_in, expert_gate, expert_up, expert_down):
    gate_val = jnp.einsum(
        "sjcd,jdf->sjcf", slots_in, expert_gate, preferred_element_type=jnp.float32
    )
    up_val = jnp.einsum("sjcd,jdf->sjcf", slots_in, expert_up, preferred_element_type=jnp.float32)
    inner = (jax.nn.silu(gate_val) * up_val).astype(jnp.bfloat16)
    return jnp.einsum("sjcf,jfd->sjcd", inner, expert_down, preferred_element_type=jnp.float32)


def body(
    hidden,
    norm_gain,
    shared_gate,
    shared_up,
    shared_down,
    expert_gate,
    expert_up,
    expert_down,
    adapter_in,
    adapter_out,
    active,
    lengths,
    request_adapter,
    routes,
    route_weights,
):
    tok_rows = routes.shape[0]
    top_count = routes.shape[1]
    dp_count = lax.axis_size("dp")
    mp_count = lax.axis_size("mp")
    dp_index = lax.axis_index("dp")
    local_experts = expert_gate.shape[0]
    total_experts = local_experts * dp_count
    capacity = mp_count * max(1, tok_rows * top_count * 4 // (total_experts * mp_count * 3))

    active_count = active.shape[0]
    rank_width = adapter_in.shape[2]
    local_adapters = adapter_in.shape[0]
    owned_ids = dp_index * local_adapters + jnp.arange(local_adapters, dtype=jnp.int32)
    selector = (active[:, None] == owned_ids[None, :]).astype(jnp.bfloat16)
    picked_in = jnp.einsum(
        "ji,isr->jsr", selector, adapter_in, preferred_element_type=jnp.float32
    ).astype(jnp.bfloat16)
    picked_out = jnp.einsum(
        "ji,ird->jrd", selector, adapter_out, preferred_element_type=jnp.float32
    ).astype(jnp.bfloat16)
    picked_in, picked_out = lax.psum((picked_in, picked_out), "dp")

    gathered = lax.all_gather(hidden, "mp", axis=1, tiled=True)
    values = gathered.astype(jnp.float32)
    factor = lax.rsqrt(jnp.mean(values * values, axis=-1, keepdims=True) + 1e-06)
    normed = (values * factor * norm_gain.astype(jnp.float32)).astype(jnp.bfloat16)
    width = normed.shape[1]
    shared_lin = jnp.dot(normed, shared_gate, preferred_element_type=jnp.float32)
    shared_pre = jnp.dot(normed, shared_up, preferred_element_type=jnp.float32)
    shared_act = (jax.nn.silu(shared_lin) * shared_pre).astype(jnp.bfloat16)

    request_end = jnp.cumsum(lengths)
    positions = dp_index * tok_rows + jnp.arange(tok_rows, dtype=jnp.int32)
    request_of = jnp.sum((request_end[None, :] <= positions[:, None]).astype(jnp.int32), axis=1)
    request_hot = (
        request_of[:, None] == jnp.arange(lengths.shape[0], dtype=jnp.int32)[None, :]
    ).astype(jnp.int32)
    slot_of = jnp.sum(request_hot * request_adapter[None, :], axis=1)
    chosen = (slot_of[:, None] == jnp.arange(active_count, dtype=jnp.int32)[None, :]).astype(
        jnp.float32
    )
    in_matrix = jnp.transpose(picked_in, (1, 0, 2)).reshape(
        shared_act.shape[1], active_count * rank_width
    )
    lowrank = jnp.dot(shared_act, in_matrix, preferred_element_type=jnp.float32)
    lowrank = (lowrank.reshape(tok_rows, active_count, rank_width) * chosen[:, :, None]).reshape(
        tok_rows, active_count * rank_width
    )
    adapted = jnp.dot(
        lowrank,
        picked_out.reshape(active_count * rank_width, width).astype(jnp.float32),
        precision=lax.Precision.HIGHEST,
    )

    flat_routes = routes.reshape(-1)
    expert_hot = (
        flat_routes[:, None] == jnp.arange(total_experts, dtype=jnp.int32)[None, :]
    ).astype(jnp.int32)
    earlier = jnp.cumsum(expert_hot, axis=0) - expert_hot
    position = jnp.sum(earlier * expert_hot, axis=1)
    slot_index = (flat_routes * capacity + position).reshape(tok_rows, top_count)
    slot_count = total_experts * capacity
    slot_hit = slot_index[:, :, None] == jnp.arange(slot_count, dtype=jnp.int32)[None, None, :]
    dispatch = jnp.any(slot_hit, axis=1).astype(jnp.bfloat16)
    send_rows = jnp.einsum(
        "ts,td->sd", dispatch, normed, preferred_element_type=jnp.float32
    ).astype(jnp.bfloat16)
    send_rows = send_rows.reshape(dp_count, local_experts, capacity, width)
    returned = lax.all_to_all(
        experts_apply(
            lax.all_to_all(send_rows, "dp", split_axis=0, concat_axis=0, tiled=True),
            expert_gate,
            expert_up,
            expert_down,
        ).astype(jnp.bfloat16),
        "dp",
        split_axis=0,
        concat_axis=0,
        tiled=True,
    )
    returned = returned.reshape(slot_count, width)
    combine = jnp.sum(
        jnp.where(slot_hit, route_weights[:, :, None], 0.0), axis=1
    )
    combine_hi = combine.astype(jnp.bfloat16)
    combine_lo = (combine - combine_hi.astype(jnp.float32)).astype(jnp.bfloat16)
    routed = jnp.dot(combine_hi, returned, preferred_element_type=jnp.float32) + jnp.dot(
        combine_lo, returned, preferred_element_type=jnp.float32
    )

    partial_out = (
        jnp.dot(shared_act, shared_down, preferred_element_type=jnp.float32) + adapted + routed
    )
    return lax.psum_scatter(partial_out.astype(jnp.bfloat16), "mp", scatter_dimension=1, tiled=True)


def solution(mesh):
    in_specs = (
        P("dp", "mp"),
        P(),
        P(None, "mp"),
        P(None, "mp"),
        P("mp", None),
        P("dp", None, "mp"),
        P("dp", None, "mp"),
        P("dp", "mp", None),
        P("dp", "mp", None),
        P("dp", None, None),
        P(),
        P(),
        P(),
        P("dp", None),
        P("dp", None),
    )
    out_specs = P("dp", "mp")
    return jax.shard_map(body, mesh=mesh, in_specs=in_specs, out_specs=out_specs, check_vma=False)
```

```python
import jax
import jax.numpy as jnp
from jax import lax
from jax.sharding import PartitionSpec as P


def body(
    hidden,
    norm_gain,
    shared_gate,
    shared_up,
    shared_down,
    expert_gate,
    expert_up,
    expert_down,
    adapter_in,
    adapter_out,
    active,
    lengths,
    request_adapter,
    routes,
    route_weights,
):
    tok_rows = routes.shape[0]
    top_count = routes.shape[1]
    dp_count = lax.axis_size("dp")
    mp_count = lax.axis_size("mp")
    dp_index = lax.axis_index("dp")
    local_experts = expert_gate.shape[0]
    total_experts = local_experts * dp_count
    capacity = mp_count * max(1, tok_rows * top_count * 4 // (total_experts * mp_count * 3))

    active_count = active.shape[0]
    rank_width = adapter_in.shape[2]
    local_adapters = adapter_in.shape[0]
    owned_ids = dp_index * local_adapters + jnp.arange(local_adapters, dtype=jnp.int32)
    selector = (active[:, None] == owned_ids[None, :]).astype(jnp.bfloat16)
    picked_in = jnp.einsum(
        "ji,isr->jsr", selector, adapter_in, preferred_element_type=jnp.float32
    ).astype(jnp.bfloat16)
    picked_out = jnp.einsum(
        "ji,ird->jrd", selector, adapter_out, preferred_element_type=jnp.float32
    ).astype(jnp.bfloat16)
    picked_in, picked_out = lax.psum((picked_in, picked_out), "dp")

    gathered = lax.all_gather(hidden, "mp", axis=1, tiled=True)
    values = gathered.astype(jnp.float32)
    factor = lax.rsqrt(jnp.mean(values * values, axis=-1, keepdims=True) + 1e-06)
    normed = (values * factor * norm_gain.astype(jnp.float32)).astype(jnp.bfloat16)
    width = normed.shape[1]
    shared_lin = jnp.dot(normed, shared_gate, preferred_element_type=jnp.float32)
    shared_pre = jnp.dot(normed, shared_up, preferred_element_type=jnp.float32)
    shared_act = (jax.nn.silu(shared_lin) * shared_pre).astype(jnp.bfloat16)

    request_end = jnp.cumsum(lengths)
    positions = dp_index * tok_rows + jnp.arange(tok_rows, dtype=jnp.int32)
    request_of = jnp.sum((request_end[None, :] <= positions[:, None]).astype(jnp.int32), axis=1)
    request_hot = (
        request_of[:, None] == jnp.arange(lengths.shape[0], dtype=jnp.int32)[None, :]
    ).astype(jnp.int32)
    slot_of = jnp.sum(request_hot * request_adapter[None, :], axis=1)
    chosen = (slot_of[:, None] == jnp.arange(active_count, dtype=jnp.int32)[None, :]).astype(
        jnp.float32
    )
    in_matrix = jnp.transpose(picked_in, (1, 0, 2)).reshape(
        shared_act.shape[1], active_count * rank_width
    )
    lowrank = jnp.dot(shared_act, in_matrix, preferred_element_type=jnp.float32)
    lowrank = (lowrank.reshape(tok_rows, active_count, rank_width) * chosen[:, :, None]).reshape(
        tok_rows, active_count * rank_width
    )
    adapted = jnp.dot(
        lowrank,
        picked_out.reshape(active_count * rank_width, width).astype(jnp.float32),
        precision=lax.Precision.HIGHEST,
    )

    flat_routes = routes.reshape(-1)
    expert_hot = (
        flat_routes[:, None] == jnp.arange(total_experts, dtype=jnp.int32)[None, :]
    ).astype(jnp.int32)
    earlier = jnp.cumsum(expert_hot, axis=0) - expert_hot
    position = jnp.sum(earlier * expert_hot, axis=1)
    chunk_rows = dp_count * capacity
    slot_index = (
        (flat_routes % local_experts) * chunk_rows
        + (flat_routes // local_experts) * capacity
        + position
    ).reshape(tok_rows, top_count)
    slot_count = total_experts * capacity
    slot_hit = slot_index[:, :, None] == jnp.arange(slot_count, dtype=jnp.int32)[None, None, :]
    dispatch = jnp.any(slot_hit, axis=1).astype(jnp.bfloat16)
    send_rows = jnp.einsum(
        "ts,td->sd", dispatch, normed, preferred_element_type=jnp.float32
    ).astype(jnp.bfloat16)
    send_rows = send_rows.reshape(local_experts, dp_count, capacity, width)
    pieces = []
    for j in range(local_experts):
        rows_in = lax.all_to_all(send_rows[j], "dp", split_axis=0, concat_axis=0, tiled=True)
        rows_in = rows_in.reshape(chunk_rows, width)
        gate_val = jnp.dot(rows_in, expert_gate[j], preferred_element_type=jnp.float32)
        up_val = jnp.dot(rows_in, expert_up[j], preferred_element_type=jnp.float32)
        inner = (jax.nn.silu(gate_val) * up_val).astype(jnp.bfloat16)
        rows_out = jnp.dot(inner, expert_down[j], preferred_element_type=jnp.float32)
        rows_out = rows_out.astype(jnp.bfloat16).reshape(dp_count, capacity, width)
        pieces.append(lax.all_to_all(rows_out, "dp", split_axis=0, concat_axis=0, tiled=True))
    combine = jnp.sum(
        jnp.where(slot_hit, route_weights[:, :, None], 0.0), axis=1
    )
    combine_hi = combine.astype(jnp.bfloat16)
    combine_lo = (combine - combine_hi.astype(jnp.float32)).astype(jnp.bfloat16)
    routed = None
    for j, piece in enumerate(pieces):
        piece = piece.reshape(chunk_rows, width)
        cols = slice(j * chunk_rows, (j + 1) * chunk_rows)
        part = jnp.dot(combine_hi[:, cols], piece, preferred_element_type=jnp.float32) + jnp.dot(
            combine_lo[:, cols], piece, preferred_element_type=jnp.float32
        )
        routed = part if routed is None else routed + part

    partial_out = (
        jnp.dot(shared_act, shared_down, preferred_element_type=jnp.float32) + adapted + routed
    )
    return lax.psum_scatter(partial_out.astype(jnp.bfloat16), "mp", scatter_dimension=1, tiled=True)


def solution(mesh):
    in_specs = (
        P("dp", "mp"),
        P(),
        P(None, "mp"),
        P(None, "mp"),
        P("mp", None),
        P("dp", None, "mp"),
        P("dp", None, "mp"),
        P("dp", "mp", None),
        P("dp", "mp", None),
        P("dp", None, None),
        P(),
        P(),
        P(),
        P("dp", None),
        P("dp", None),
    )
    out_specs = P("dp", "mp")
    return jax.shard_map(body, mesh=mesh, in_specs=in_specs, out_specs=out_specs, check_vma=False)
```

```python
import jax
import jax.numpy as jnp
from jax import lax
from jax.sharding import PartitionSpec as P


def experts_apply(slots_in, expert_gate, expert_up, expert_down):
    gate_val = jnp.einsum(
        "sjcd,jdf->sjcf", slots_in, expert_gate, preferred_element_type=jnp.float32
    )
    up_val = jnp.einsum("sjcd,jdf->sjcf", slots_in, expert_up, preferred_element_type=jnp.float32)
    inner = (jax.nn.silu(gate_val) * up_val).astype(jnp.bfloat16)
    return jnp.einsum("sjcf,jfd->sjcd", inner, expert_down, preferred_element_type=jnp.float32)


def body(
    hidden,
    norm_gain,
    shared_gate,
    shared_up,
    shared_down,
    expert_gate,
    expert_up,
    expert_down,
    adapter_in,
    adapter_out,
    active,
    lengths,
    request_adapter,
    routes,
    route_weights,
):
    tok_rows = routes.shape[0]
    top_count = routes.shape[1]
    dp_count = lax.axis_size("dp")
    mp_count = lax.axis_size("mp")
    dp_index = lax.axis_index("dp")
    local_experts = expert_gate.shape[0]
    total_experts = local_experts * dp_count
    capacity = mp_count * max(1, tok_rows * top_count * 4 // (total_experts * mp_count * 3))

    active_count = active.shape[0]
    rank_width = adapter_in.shape[2]
    local_adapters = adapter_in.shape[0]
    owned_ids = dp_index * local_adapters + jnp.arange(local_adapters, dtype=jnp.int32)
    selector = (active[:, None] == owned_ids[None, :]).astype(jnp.bfloat16)
    picked_in = jnp.einsum(
        "ji,isr->jsr", selector, adapter_in, preferred_element_type=jnp.float32
    ).astype(jnp.bfloat16)
    picked_out = jnp.einsum(
        "ji,ird->jrd", selector, adapter_out, preferred_element_type=jnp.float32
    ).astype(jnp.bfloat16)
    picked_in, picked_out = lax.psum((picked_in, picked_out), "dp")

    gathered = lax.all_gather(hidden, "mp", axis=1, tiled=True)
    values = gathered.astype(jnp.float32)
    factor = lax.rsqrt(jnp.mean(values * values, axis=-1, keepdims=True) + 1e-06)
    normed = (values * factor * norm_gain.astype(jnp.float32)).astype(jnp.bfloat16)
    width = normed.shape[1]
    shared_lin = jnp.dot(normed, shared_gate, preferred_element_type=jnp.float32)
    shared_pre = jnp.dot(normed, shared_up, preferred_element_type=jnp.float32)
    shared_act = (jax.nn.silu(shared_lin) * shared_pre).astype(jnp.bfloat16)

    request_end = jnp.cumsum(lengths)
    positions = dp_index * tok_rows + jnp.arange(tok_rows, dtype=jnp.int32)
    request_of = jnp.sum((request_end[None, :] <= positions[:, None]).astype(jnp.int32), axis=1)
    request_hot = (
        request_of[:, None] == jnp.arange(lengths.shape[0], dtype=jnp.int32)[None, :]
    ).astype(jnp.int32)
    slot_of = jnp.sum(request_hot * request_adapter[None, :], axis=1)
    chosen = (slot_of[:, None] == jnp.arange(active_count, dtype=jnp.int32)[None, :]).astype(
        jnp.float32
    )
    in_matrix = jnp.transpose(picked_in, (1, 0, 2)).reshape(
        shared_act.shape[1], active_count * rank_width
    )
    lowrank = jnp.dot(shared_act, in_matrix, preferred_element_type=jnp.float32)
    lowrank = (lowrank.reshape(tok_rows, active_count, rank_width) * chosen[:, :, None]).reshape(
        tok_rows, active_count * rank_width
    )
    adapted = jnp.dot(
        lowrank,
        picked_out.reshape(active_count * rank_width, width).astype(jnp.float32),
        precision=lax.Precision.HIGHEST,
    )

    flat_routes = routes.reshape(-1)
    expert_hot = (
        flat_routes[:, None] == jnp.arange(total_experts, dtype=jnp.int32)[None, :]
    ).astype(jnp.int32)
    earlier = jnp.cumsum(expert_hot, axis=0) - expert_hot
    position = jnp.sum(earlier * expert_hot, axis=1)
    slot_index = (flat_routes * capacity + position).reshape(tok_rows, top_count)
    slot_count = total_experts * capacity
    slot_hit = slot_index[:, :, None] == jnp.arange(slot_count, dtype=jnp.int32)[None, None, :]
    dispatch = jnp.any(slot_hit, axis=1).astype(jnp.bfloat16)
    send_rows = jnp.einsum(
        "ts,td->sd", dispatch, normed, preferred_element_type=jnp.float32
    ).astype(jnp.bfloat16)
    send_rows = send_rows.reshape(dp_count, local_experts, capacity, width)
    rows_out = experts_apply(
        lax.all_to_all(send_rows, "dp", split_axis=0, concat_axis=0, tiled=True),
        expert_gate,
        expert_up,
        expert_down,
    ).astype(jnp.bfloat16)
    col_width = width // mp_count
    rows_out = rows_out.reshape(dp_count, local_experts, capacity, mp_count, col_width)
    rows_out = jnp.transpose(rows_out, (0, 3, 1, 2, 4)).reshape(
        dp_count * mp_count, local_experts * capacity, col_width
    )
    returned = lax.all_to_all(rows_out, ("dp", "mp"), split_axis=0, concat_axis=0, tiled=True)
    returned = returned.reshape(dp_count, mp_count, local_experts * capacity, col_width)
    returned = jnp.sum(returned.astype(jnp.float32), axis=1).reshape(slot_count, col_width)
    combine = jnp.sum(
        jnp.where(slot_hit, route_weights[:, :, None], 0.0), axis=1
    )
    routed = jnp.dot(combine, returned, precision=lax.Precision.HIGHEST)

    shared_part = jnp.dot(shared_act, shared_down, preferred_element_type=jnp.float32) + adapted
    shared_part = lax.psum_scatter(shared_part, "mp", scatter_dimension=1, tiled=True)
    return (shared_part + routed).astype(jnp.bfloat16)


def solution(mesh):
    in_specs = (
        P("dp", "mp"),
        P(),
        P(None, "mp"),
        P(None, "mp"),
        P("mp", None),
        P("dp", None, "mp"),
        P("dp", None, "mp"),
        P("dp", "mp", None),
        P("dp", "mp", None),
        P("dp", None, None),
        P(),
        P(),
        P(),
        P("dp", None),
        P("dp", None),
    )
    out_specs = P("dp", "mp")
    return jax.shard_map(body, mesh=mesh, in_specs=in_specs, out_specs=out_specs, check_vma=False)
```

```python
import jax
import jax.numpy as jnp
from jax import lax
from jax.experimental import pallas as pl
from jax.experimental.pallas import tpu as pltpu
from jax.sharding import PartitionSpec as P


def _expert_kernel(x_ref, wg_ref, wu_ref, wd_ref, o_ref, inner_ref):
    @pl.when(pl.program_id(1) == 0)
    def _():
        x = x_ref[...]
        x = x.reshape(x.shape[0] * x.shape[1], x.shape[2])
        g = jnp.dot(x, wg_ref[...], preferred_element_type=jnp.float32)
        u = jnp.dot(x, wu_ref[...], preferred_element_type=jnp.float32)
        inner_ref[...] = (g / (1.0 + jnp.exp(-g)) * u).astype(inner_ref.dtype)

    out = jnp.dot(inner_ref[...], wd_ref[...], preferred_element_type=jnp.float32)
    o_ref[...] = out.astype(o_ref.dtype).reshape(o_ref.shape)


def experts_kernel(rows_in, expert_gate, expert_up, expert_down, parts):
    sources, local_experts, capacity, width = rows_in.shape
    hidden = expert_gate.shape[2]
    col_width = width // parts
    rows = sources * capacity
    flops = local_experts * 6 * rows * width * hidden
    nbytes = 2 * (2 * rows_in.size + expert_gate.size + expert_up.size + expert_down.size)
    return pl.pallas_call(
        _expert_kernel,
        grid=(local_experts, parts),
        in_specs=[
            pl.BlockSpec((sources, None, capacity, width), lambda j, m: (0, j, 0, 0)),
            pl.BlockSpec((None, width, hidden), lambda j, m: (j, 0, 0)),
            pl.BlockSpec((None, width, hidden), lambda j, m: (j, 0, 0)),
            pl.BlockSpec((None, hidden, col_width), lambda j, m: (j, 0, m)),
        ],
        out_specs=pl.BlockSpec(
            (sources, None, None, capacity, col_width), lambda j, m: (0, m, j, 0, 0)
        ),
        out_shape=jax.ShapeDtypeStruct(
            (sources, parts, local_experts, capacity, col_width), jnp.bfloat16
        ),
        scratch_shapes=[pltpu.VMEM((rows, hidden), jnp.bfloat16)],
        compiler_params=pltpu.CompilerParams(dimension_semantics=("arbitrary", "arbitrary")),
        cost_estimate=pl.CostEstimate(
            flops=flops, transcendentals=local_experts * rows * hidden, bytes_accessed=nbytes
        ),
    )(rows_in, expert_gate, expert_up, expert_down)


def body(
    hidden,
    norm_gain,
    shared_gate,
    shared_up,
    shared_down,
    expert_gate,
    expert_up,
    expert_down,
    adapter_in,
    adapter_out,
    active,
    lengths,
    request_adapter,
    routes,
    route_weights,
):
    tok_rows = routes.shape[0]
    top_count = routes.shape[1]
    dp_count = lax.axis_size("dp")
    mp_count = lax.axis_size("mp")
    dp_index = lax.axis_index("dp")
    local_experts = expert_gate.shape[0]
    total_experts = local_experts * dp_count
    capacity = mp_count * max(1, tok_rows * top_count * 4 // (total_experts * mp_count * 3))

    active_count = active.shape[0]
    rank_width = adapter_in.shape[2]
    local_adapters = adapter_in.shape[0]
    owned_ids = dp_index * local_adapters + jnp.arange(local_adapters, dtype=jnp.int32)
    selector = (active[:, None] == owned_ids[None, :]).astype(jnp.bfloat16)
    picked_in = jnp.einsum(
        "ji,isr->jsr", selector, adapter_in, preferred_element_type=jnp.float32
    ).astype(jnp.bfloat16)
    picked_out = jnp.einsum(
        "ji,ird->jrd", selector, adapter_out, preferred_element_type=jnp.float32
    ).astype(jnp.bfloat16)
    picked_in, picked_out = lax.psum((picked_in, picked_out), "dp")

    gathered = lax.all_gather(hidden, "mp", axis=1, tiled=True)
    values = gathered.astype(jnp.float32)
    factor = lax.rsqrt(jnp.mean(values * values, axis=-1, keepdims=True) + 1e-06)
    normed = (values * factor * norm_gain.astype(jnp.float32)).astype(jnp.bfloat16)
    width = normed.shape[1]
    shared_lin = jnp.dot(normed, shared_gate, preferred_element_type=jnp.float32)
    shared_pre = jnp.dot(normed, shared_up, preferred_element_type=jnp.float32)
    shared_act = (jax.nn.silu(shared_lin) * shared_pre).astype(jnp.bfloat16)

    request_end = jnp.cumsum(lengths)
    positions = dp_index * tok_rows + jnp.arange(tok_rows, dtype=jnp.int32)
    request_of = jnp.sum((request_end[None, :] <= positions[:, None]).astype(jnp.int32), axis=1)
    request_hot = (
        request_of[:, None] == jnp.arange(lengths.shape[0], dtype=jnp.int32)[None, :]
    ).astype(jnp.int32)
    slot_of = jnp.sum(request_hot * request_adapter[None, :], axis=1)
    chosen = (slot_of[:, None] == jnp.arange(active_count, dtype=jnp.int32)[None, :]).astype(
        jnp.float32
    )
    in_matrix = jnp.transpose(picked_in, (1, 0, 2)).reshape(
        shared_act.shape[1], active_count * rank_width
    )
    lowrank = jnp.dot(shared_act, in_matrix, preferred_element_type=jnp.float32)
    lowrank = (lowrank.reshape(tok_rows, active_count, rank_width) * chosen[:, :, None]).reshape(
        tok_rows, active_count * rank_width
    )
    adapted = jnp.dot(
        lowrank,
        picked_out.reshape(active_count * rank_width, width).astype(jnp.float32),
        precision=lax.Precision.HIGHEST,
    )

    flat_routes = routes.reshape(-1)
    expert_hot = (
        flat_routes[:, None] == jnp.arange(total_experts, dtype=jnp.int32)[None, :]
    ).astype(jnp.int32)
    earlier = jnp.cumsum(expert_hot, axis=0) - expert_hot
    position = jnp.sum(earlier * expert_hot, axis=1)
    slot_index = (flat_routes * capacity + position).reshape(tok_rows, top_count)
    slot_count = total_experts * capacity
    slot_hit = slot_index[:, :, None] == jnp.arange(slot_count, dtype=jnp.int32)[None, None, :]
    dispatch = jnp.any(slot_hit, axis=1).astype(jnp.bfloat16)
    send_rows = jnp.einsum(
        "ts,td->sd", dispatch, normed, preferred_element_type=jnp.float32
    ).astype(jnp.bfloat16)
    send_rows = send_rows.reshape(dp_count, local_experts, capacity, width)
    rows_out = experts_kernel(
        lax.all_to_all(send_rows, "dp", split_axis=0, concat_axis=0, tiled=True),
        expert_gate,
        expert_up,
        expert_down,
        mp_count,
    )
    col_width = width // mp_count
    rows_out = rows_out.reshape(dp_count * mp_count, local_experts * capacity, col_width)
    returned = lax.all_to_all(rows_out, ("dp", "mp"), split_axis=0, concat_axis=0, tiled=True)
    returned = returned.reshape(dp_count, mp_count, local_experts * capacity, col_width)
    returned = jnp.sum(returned.astype(jnp.float32), axis=1).reshape(slot_count, col_width)
    combine = jnp.sum(
        jnp.where(slot_hit, route_weights[:, :, None], 0.0), axis=1
    )
    routed = jnp.dot(combine, returned, precision=lax.Precision.HIGHEST)

    shared_part = jnp.dot(shared_act, shared_down, preferred_element_type=jnp.float32) + adapted
    shared_part = lax.psum_scatter(
        shared_part.astype(jnp.bfloat16), "mp", scatter_dimension=1, tiled=True
    )
    return (shared_part.astype(jnp.float32) + routed).astype(jnp.bfloat16)


def solution(mesh):
    in_specs = (
        P("dp", "mp"),
        P(),
        P(None, "mp"),
        P(None, "mp"),
        P("mp", None),
        P("dp", None, "mp"),
        P("dp", None, "mp"),
        P("dp", "mp", None),
        P("dp", "mp", None),
        P("dp", None, None),
        P(),
        P(),
        P(),
        P("dp", None),
        P("dp", None),
    )
    out_specs = P("dp", "mp")
    return jax.shard_map(body, mesh=mesh, in_specs=in_specs, out_specs=out_specs, check_vma=False)
```

```python
import jax
import jax.numpy as jnp
from jax import lax
from jax.experimental import pallas as pl
from jax.experimental.pallas import tpu as pltpu
from jax.sharding import PartitionSpec as P


def _expert_kernel(x_ref, wg_ref, wu_ref, wd_ref, o_ref, inner_ref):
    @pl.when(pl.program_id(1) == 0)
    def _():
        x = x_ref[...]
        x = x.reshape(x.shape[0] * x.shape[1], x.shape[2])
        g = jnp.dot(x, wg_ref[...], preferred_element_type=jnp.float32)
        u = jnp.dot(x, wu_ref[...], preferred_element_type=jnp.float32)
        inner_ref[...] = (g / (1.0 + jnp.exp(-g)) * u).astype(inner_ref.dtype)

    out = jnp.dot(inner_ref[...], wd_ref[...], preferred_element_type=jnp.float32)
    o_ref[...] = out.astype(o_ref.dtype).reshape(o_ref.shape)


def experts_kernel(rows_in, expert_gate, expert_up, expert_down, parts):
    sources, local_experts, capacity, width = rows_in.shape
    hidden = expert_gate.shape[2]
    col_width = width // parts
    rows = sources * capacity
    flops = local_experts * 6 * rows * width * hidden
    nbytes = 2 * (2 * rows_in.size + expert_gate.size + expert_up.size + expert_down.size)
    return pl.pallas_call(
        _expert_kernel,
        grid=(local_experts, parts),
        in_specs=[
            pl.BlockSpec((sources, None, capacity, width), lambda j, m: (0, j, 0, 0)),
            pl.BlockSpec((None, width, hidden), lambda j, m: (j, 0, 0)),
            pl.BlockSpec((None, width, hidden), lambda j, m: (j, 0, 0)),
            pl.BlockSpec((None, hidden, col_width), lambda j, m: (j, 0, m)),
        ],
        out_specs=pl.BlockSpec(
            (sources, None, None, capacity, col_width), lambda j, m: (0, m, j, 0, 0)
        ),
        out_shape=jax.ShapeDtypeStruct(
            (sources, parts, local_experts, capacity, col_width), jnp.bfloat16
        ),
        scratch_shapes=[pltpu.VMEM((rows, hidden), jnp.bfloat16)],
        compiler_params=pltpu.CompilerParams(dimension_semantics=("arbitrary", "arbitrary")),
        cost_estimate=pl.CostEstimate(
            flops=flops, transcendentals=local_experts * rows * hidden, bytes_accessed=nbytes
        ),
    )(rows_in, expert_gate, expert_up, expert_down)


def body(
    hidden,
    norm_gain,
    shared_gate,
    shared_up,
    shared_down,
    expert_gate,
    expert_up,
    expert_down,
    adapter_in,
    adapter_out,
    active,
    lengths,
    request_adapter,
    routes,
    route_weights,
):
    tok_rows = routes.shape[0]
    top_count = routes.shape[1]
    dp_count = lax.axis_size("dp")
    mp_count = lax.axis_size("mp")
    dp_index = lax.axis_index("dp")
    mp_index = lax.axis_index("mp")
    col_width = hidden.shape[1]
    local_experts = expert_gate.shape[0]
    total_experts = local_experts * dp_count
    capacity = mp_count * max(1, tok_rows * top_count * 4 // (total_experts * mp_count * 3))

    active_count = active.shape[0]
    rank_width = adapter_in.shape[2]
    local_adapters = adapter_in.shape[0]
    owned_ids = dp_index * local_adapters + jnp.arange(local_adapters, dtype=jnp.int32)
    selector = (active[:, None] == owned_ids[None, :]).astype(jnp.bfloat16)
    picked_in = jnp.einsum(
        "ji,isr->jsr", selector, adapter_in, preferred_element_type=jnp.float32
    ).astype(jnp.bfloat16)
    out_cols = lax.dynamic_slice_in_dim(adapter_out, mp_index * col_width, col_width, axis=2)
    picked_out = jnp.einsum(
        "ji,ird->jrd", selector, out_cols, preferred_element_type=jnp.float32
    ).astype(jnp.bfloat16)
    picked_in, picked_out = lax.psum((picked_in, picked_out), "dp")

    gathered = lax.all_gather(hidden, "mp", axis=1, tiled=True)
    values = gathered.astype(jnp.float32)
    factor = lax.rsqrt(jnp.mean(values * values, axis=-1, keepdims=True) + 1e-06)
    normed = (values * factor * norm_gain.astype(jnp.float32)).astype(jnp.bfloat16)
    width = normed.shape[1]
    shared_lin = jnp.dot(normed, shared_gate, preferred_element_type=jnp.float32)
    shared_pre = jnp.dot(normed, shared_up, preferred_element_type=jnp.float32)
    shared_act = (jax.nn.silu(shared_lin) * shared_pre).astype(jnp.bfloat16)

    request_end = jnp.cumsum(lengths)
    positions = dp_index * tok_rows + jnp.arange(tok_rows, dtype=jnp.int32)
    request_of = jnp.sum((request_end[None, :] <= positions[:, None]).astype(jnp.int32), axis=1)
    request_hot = (
        request_of[:, None] == jnp.arange(lengths.shape[0], dtype=jnp.int32)[None, :]
    ).astype(jnp.int32)
    slot_of = jnp.sum(request_hot * request_adapter[None, :], axis=1)
    chosen = (slot_of[:, None] == jnp.arange(active_count, dtype=jnp.int32)[None, :]).astype(
        jnp.float32
    )
    in_matrix = jnp.transpose(picked_in, (1, 0, 2)).reshape(
        shared_act.shape[1], active_count * rank_width
    )
    lowrank = jnp.dot(shared_act, in_matrix, preferred_element_type=jnp.float32)
    lowrank_sel = jnp.sum(
        lowrank.reshape(tok_rows, active_count, rank_width) * chosen[:, :, None], axis=1
    )
    lowrank_sel = lax.psum(lowrank_sel, "mp")
    lowrank = (chosen[:, :, None] * lowrank_sel[:, None, :]).reshape(
        tok_rows, active_count * rank_width
    )
    adapted = jnp.dot(
        lowrank,
        picked_out.reshape(active_count * rank_width, col_width).astype(jnp.float32),
        precision=lax.Precision.HIGHEST,
    )

    flat_routes = routes.reshape(-1)
    expert_hot = (
        flat_routes[:, None] == jnp.arange(total_experts, dtype=jnp.int32)[None, :]
    ).astype(jnp.int32)
    earlier = jnp.cumsum(expert_hot, axis=0) - expert_hot
    position = jnp.sum(earlier * expert_hot, axis=1)
    slot_index = (flat_routes * capacity + position).reshape(tok_rows, top_count)
    slot_count = total_experts * capacity
    slot_hit = slot_index[:, :, None] == jnp.arange(slot_count, dtype=jnp.int32)[None, None, :]
    dispatch = jnp.any(slot_hit, axis=1).astype(jnp.bfloat16)
    send_rows = jnp.einsum(
        "ts,td->sd", dispatch, normed, preferred_element_type=jnp.float32
    ).astype(jnp.bfloat16)
    send_rows = send_rows.reshape(dp_count, local_experts, capacity, width)
    rows_out = experts_kernel(
        lax.all_to_all(send_rows, "dp", split_axis=0, concat_axis=0, tiled=True),
        expert_gate,
        expert_up,
        expert_down,
        mp_count,
    )
    rows_out = rows_out.reshape(dp_count * mp_count, local_experts * capacity, col_width)
    returned = lax.all_to_all(rows_out, ("dp", "mp"), split_axis=0, concat_axis=0, tiled=True)
    returned = returned.reshape(dp_count, mp_count, local_experts * capacity, col_width)
    returned = jnp.sum(returned.astype(jnp.float32), axis=1).reshape(slot_count, col_width)
    combine = jnp.sum(
        jnp.where(slot_hit, route_weights[:, :, None], 0.0), axis=1
    )
    routed = jnp.dot(combine, returned, precision=lax.Precision.HIGHEST)

    shared_part = jnp.dot(shared_act, shared_down, preferred_element_type=jnp.float32)
    shared_part = shared_part.astype(jnp.bfloat16).reshape(tok_rows, mp_count, col_width)
    shared_part = lax.all_to_all(
        jnp.transpose(shared_part, (1, 0, 2)), "mp", split_axis=0, concat_axis=0, tiled=True
    )
    shared_part = jnp.sum(shared_part.astype(jnp.float32), axis=0)
    return (shared_part + adapted + routed).astype(jnp.bfloat16)


def solution(mesh):
    in_specs = (
        P("dp", "mp"),
        P(),
        P(None, "mp"),
        P(None, "mp"),
        P("mp", None),
        P("dp", None, "mp"),
        P("dp", None, "mp"),
        P("dp", "mp", None),
        P("dp", "mp", None),
        P("dp", None, None),
        P(),
        P(),
        P(),
        P("dp", None),
        P("dp", None),
    )
    out_specs = P("dp", "mp")
    return jax.shard_map(body, mesh=mesh, in_specs=in_specs, out_specs=out_specs, check_vma=False)
```

```python
import jax
import jax.numpy as jnp
from jax import lax
from jax.experimental import pallas as pl
from jax.experimental.pallas import tpu as pltpu
from jax.sharding import PartitionSpec as P


def _expert_kernel(x_ref, wg_ref, wu_ref, wd_ref, o_ref, inner_ref):
    @pl.when(pl.program_id(1) == 0)
    def _():
        x = x_ref[...]
        x = x.reshape(x.shape[0] * x.shape[1], x.shape[2])
        g = jnp.dot(x, wg_ref[...], preferred_element_type=jnp.float32)
        u = jnp.dot(x, wu_ref[...], preferred_element_type=jnp.float32)
        inner_ref[...] = (g / (1.0 + jnp.exp(-g)) * u).astype(inner_ref.dtype)

    out = jnp.dot(inner_ref[...], wd_ref[...], preferred_element_type=jnp.float32)
    o_ref[...] = out.astype(o_ref.dtype).reshape(o_ref.shape)


def experts_kernel(rows_in, expert_gate, expert_up, expert_down, parts):
    sources, local_experts, capacity, width = rows_in.shape
    hidden = expert_gate.shape[2]
    col_width = width // parts
    rows = sources * capacity
    flops = local_experts * 6 * rows * width * hidden
    nbytes = 2 * (2 * rows_in.size + expert_gate.size + expert_up.size + expert_down.size)
    return pl.pallas_call(
        _expert_kernel,
        grid=(local_experts, parts),
        in_specs=[
            pl.BlockSpec((sources, None, capacity, width), lambda j, m: (0, j, 0, 0)),
            pl.BlockSpec((None, width, hidden), lambda j, m: (j, 0, 0)),
            pl.BlockSpec((None, width, hidden), lambda j, m: (j, 0, 0)),
            pl.BlockSpec((None, hidden, col_width), lambda j, m: (j, 0, m)),
        ],
        out_specs=pl.BlockSpec(
            (sources, None, None, capacity, col_width), lambda j, m: (0, m, j, 0, 0)
        ),
        out_shape=jax.ShapeDtypeStruct(
            (sources, parts, local_experts, capacity, col_width), jnp.bfloat16
        ),
        scratch_shapes=[pltpu.VMEM((rows, hidden), jnp.bfloat16)],
        compiler_params=pltpu.CompilerParams(dimension_semantics=("arbitrary", "arbitrary")),
        cost_estimate=pl.CostEstimate(
            flops=flops, transcendentals=local_experts * rows * hidden, bytes_accessed=nbytes
        ),
    )(rows_in, expert_gate, expert_up, expert_down)


def body(
    hidden,
    norm_gain,
    shared_gate,
    shared_up,
    shared_down,
    expert_gate,
    expert_up,
    expert_down,
    adapter_in,
    adapter_out,
    active,
    lengths,
    request_adapter,
    routes,
    route_weights,
):
    tok_rows = routes.shape[0]
    top_count = routes.shape[1]
    dp_count = lax.axis_size("dp")
    mp_count = lax.axis_size("mp")
    dp_index = lax.axis_index("dp")
    mp_index = lax.axis_index("mp")
    col_width = hidden.shape[1]
    local_experts = expert_gate.shape[0]
    total_experts = local_experts * dp_count
    capacity = mp_count * max(1, tok_rows * top_count * 4 // (total_experts * mp_count * 3))

    active_count = active.shape[0]
    rank_width = adapter_in.shape[2]
    local_adapters = adapter_in.shape[0]
    owned_ids = dp_index * local_adapters + jnp.arange(local_adapters, dtype=jnp.int32)
    selector = (active[:, None] == owned_ids[None, :]).astype(jnp.bfloat16)
    picked_in = jnp.einsum(
        "ji,isr->jsr", selector, adapter_in, preferred_element_type=jnp.float32
    ).astype(jnp.bfloat16)
    out_cols = lax.dynamic_slice_in_dim(adapter_out, mp_index * col_width, col_width, axis=2)
    picked_out = jnp.einsum(
        "ji,ird->jrd", selector, out_cols, preferred_element_type=jnp.float32
    ).astype(jnp.bfloat16)
    picked_in, picked_out = lax.psum((picked_in, picked_out), "dp")

    gathered = lax.all_gather(hidden, "mp", axis=1, tiled=True)
    values = gathered.astype(jnp.float32)
    factor = lax.rsqrt(jnp.mean(values * values, axis=-1, keepdims=True) + 1e-06)
    normed = (values * factor * norm_gain.astype(jnp.float32)).astype(jnp.bfloat16)
    width = normed.shape[1]
    shared_lin = jnp.dot(normed, shared_gate, preferred_element_type=jnp.float32)
    shared_pre = jnp.dot(normed, shared_up, preferred_element_type=jnp.float32)
    shared_act = (jax.nn.silu(shared_lin) * shared_pre).astype(jnp.bfloat16)

    request_end = jnp.cumsum(lengths)
    positions = dp_index * tok_rows + jnp.arange(tok_rows, dtype=jnp.int32)
    request_of = jnp.sum((request_end[None, :] <= positions[:, None]).astype(jnp.int32), axis=1)
    request_hot = (
        request_of[:, None] == jnp.arange(lengths.shape[0], dtype=jnp.int32)[None, :]
    ).astype(jnp.int32)
    slot_of = jnp.sum(request_hot * request_adapter[None, :], axis=1)
    chosen = (slot_of[:, None] == jnp.arange(active_count, dtype=jnp.int32)[None, :]).astype(
        jnp.float32
    )
    in_matrix = jnp.transpose(picked_in, (1, 0, 2)).reshape(
        shared_act.shape[1], active_count * rank_width
    )
    lowrank = jnp.dot(shared_act, in_matrix, preferred_element_type=jnp.float32)
    lowrank_sel = jnp.sum(
        lowrank.reshape(tok_rows, active_count, rank_width) * chosen[:, :, None], axis=1
    )
    lowrank_sel = lax.psum(lowrank_sel, "mp")
    lowrank = (chosen[:, :, None] * lowrank_sel[:, None, :]).reshape(
        tok_rows, active_count * rank_width
    )
    adapted = jnp.dot(
        lowrank,
        picked_out.reshape(active_count * rank_width, col_width).astype(jnp.float32),
        precision=lax.Precision.HIGHEST,
    )

    flat_routes = routes.reshape(-1)
    expert_hot = (
        flat_routes[:, None] == jnp.arange(total_experts, dtype=jnp.int32)[None, :]
    ).astype(jnp.int32)
    earlier = jnp.cumsum(expert_hot, axis=0) - expert_hot
    position = jnp.sum(earlier * expert_hot, axis=1)
    slot_index = (flat_routes * capacity + position).reshape(tok_rows, top_count)
    slot_count = total_experts * capacity
    slot_hit = slot_index[:, :, None] == jnp.arange(slot_count, dtype=jnp.int32)[None, None, :]
    dispatch = jnp.any(slot_hit, axis=1).astype(jnp.bfloat16)
    send_rows = jnp.einsum(
        "ts,td->sd", dispatch, normed, preferred_element_type=jnp.float32
    ).astype(jnp.bfloat16)
    send_rows = send_rows.reshape(dp_count, local_experts, capacity, width)
    rows_in = lax.all_to_all(send_rows, "dp", split_axis=0, concat_axis=0, tiled=True)
    rows_out = experts_kernel(
        rows_in,
        expert_gate,
        expert_up,
        expert_down,
        mp_count,
    )
    rows_out = rows_out.reshape(dp_count * mp_count, local_experts * capacity, col_width)
    returned = lax.all_to_all(rows_out, ("dp", "mp"), split_axis=0, concat_axis=0, tiled=True)
    returned = returned.reshape(dp_count, mp_count, local_experts * capacity, col_width)
    combine = jnp.sum(
        jnp.where(slot_hit, route_weights[:, :, None], 0.0), axis=1
    )
    combine = jnp.broadcast_to(
        combine.reshape(tok_rows, dp_count, 1, local_experts * capacity),
        (tok_rows, dp_count, mp_count, local_experts * capacity),
    )
    combine_hi = combine.astype(jnp.bfloat16)
    combine_lo = (combine - combine_hi.astype(jnp.float32)).astype(jnp.bfloat16)
    routed = jnp.einsum(
        "tjms,jmsd->td", combine_hi, returned, preferred_element_type=jnp.float32
    ) + jnp.einsum("tjms,jmsd->td", combine_lo, returned, preferred_element_type=jnp.float32)

    shared_part = jnp.dot(shared_act, shared_down, preferred_element_type=jnp.float32)
    shared_part = shared_part.astype(jnp.bfloat16).reshape(tok_rows, mp_count, col_width)
    shared_part = lax.all_to_all(
        jnp.transpose(shared_part, (1, 0, 2)), "mp", split_axis=0, concat_axis=0, tiled=True
    )
    shared_part = jnp.sum(shared_part.astype(jnp.float32), axis=0)
    return (shared_part + adapted + routed).astype(jnp.bfloat16)


def solution(mesh):
    in_specs = (
        P("dp", "mp"),
        P(),
        P(None, "mp"),
        P(None, "mp"),
        P("mp", None),
        P("dp", None, "mp"),
        P("dp", None, "mp"),
        P("dp", "mp", None),
        P("dp", "mp", None),
        P("dp", None, None),
        P(),
        P(),
        P(),
        P("dp", None),
        P("dp", None),
    )
    out_specs = P("dp", "mp")

    return jax.shard_map(body, mesh=mesh, in_specs=in_specs, out_specs=out_specs, check_vma=False)
```

```python
import jax
import jax.numpy as jnp
from jax import lax
from jax.experimental import pallas as pl
from jax.experimental.pallas import tpu as pltpu
from jax.sharding import PartitionSpec as P


def _expert_kernel(x_ref, wg_ref, wu_ref, wd_ref, o_ref, inner_ref):
    @pl.when(pl.program_id(1) == 0)
    def _():
        x = x_ref[...]
        x = x.reshape(x.shape[0] * x.shape[1], x.shape[2])
        g = jnp.dot(x, wg_ref[...], preferred_element_type=jnp.float32)
        u = jnp.dot(x, wu_ref[...], preferred_element_type=jnp.float32)
        inner_ref[...] = (g / (1.0 + jnp.exp(-g)) * u).astype(inner_ref.dtype)

    out = jnp.dot(inner_ref[...], wd_ref[...], preferred_element_type=jnp.float32)
    o_ref[...] = out.astype(o_ref.dtype).reshape(o_ref.shape)


def experts_kernel(rows_in, expert_gate, expert_up, expert_down, parts):
    sources, local_experts, capacity, width = rows_in.shape
    hidden = expert_gate.shape[2]
    col_width = width // parts
    rows = sources * capacity
    flops = local_experts * 6 * rows * width * hidden
    nbytes = 2 * (2 * rows_in.size + expert_gate.size + expert_up.size + expert_down.size)
    return pl.pallas_call(
        _expert_kernel,
        grid=(local_experts, parts),
        in_specs=[
            pl.BlockSpec((sources, None, capacity, width), lambda j, m: (0, j, 0, 0)),
            pl.BlockSpec((None, width, hidden), lambda j, m: (j, 0, 0)),
            pl.BlockSpec((None, width, hidden), lambda j, m: (j, 0, 0)),
            pl.BlockSpec((None, hidden, col_width), lambda j, m: (j, 0, m)),
        ],
        out_specs=pl.BlockSpec(
            (sources, None, None, capacity, col_width), lambda j, m: (0, m, j, 0, 0)
        ),
        out_shape=jax.ShapeDtypeStruct(
            (sources, parts, local_experts, capacity, col_width), jnp.bfloat16
        ),
        scratch_shapes=[pltpu.VMEM((rows, hidden), jnp.bfloat16)],
        compiler_params=pltpu.CompilerParams(dimension_semantics=("arbitrary", "arbitrary")),
        cost_estimate=pl.CostEstimate(
            flops=flops, transcendentals=local_experts * rows * hidden, bytes_accessed=nbytes
        ),
    )(rows_in, expert_gate, expert_up, expert_down)


def body(
    hidden,
    norm_gain,
    shared_gate,
    shared_up,
    shared_down,
    expert_gate,
    expert_up,
    expert_down,
    adapter_in,
    adapter_out,
    active,
    lengths,
    request_adapter,
    routes,
    route_weights,
):
    tok_rows = routes.shape[0]
    top_count = routes.shape[1]
    dp_count = lax.axis_size("dp")
    mp_count = lax.axis_size("mp")
    dp_index = lax.axis_index("dp")
    mp_index = lax.axis_index("mp")
    col_width = hidden.shape[1]
    local_experts = expert_gate.shape[0]
    total_experts = local_experts * dp_count
    capacity = mp_count * max(1, tok_rows * top_count * 4 // (total_experts * mp_count * 3))

    active_count = active.shape[0]
    rank_width = adapter_in.shape[2]
    local_adapters = adapter_in.shape[0]
    owned_ids = dp_index * local_adapters + jnp.arange(local_adapters, dtype=jnp.int32)
    selector = (active[:, None] == owned_ids[None, :]).astype(jnp.bfloat16)
    picked_in = jnp.einsum(
        "ji,isr->jsr", selector, adapter_in, preferred_element_type=jnp.float32
    ).astype(jnp.bfloat16)
    out_cols = lax.dynamic_slice_in_dim(adapter_out, mp_index * col_width, col_width, axis=2)
    picked_out = jnp.einsum(
        "ji,ird->jrd", selector, out_cols, preferred_element_type=jnp.float32
    ).astype(jnp.bfloat16)
    picked_in, picked_out = lax.psum((picked_in, picked_out), "dp")

    shifted = [hidden] + [
        lax.ppermute(hidden, "mp", [(i, (i + k) % mp_count) for i in range(mp_count)])
        for k in range(1, mp_count)
    ]
    order = (mp_index - jnp.arange(mp_count, dtype=jnp.int32)) % mp_count
    blocks = jnp.take(jnp.stack(shifted), order, axis=0)
    gathered = jnp.transpose(blocks, (1, 0, 2)).reshape(tok_rows, mp_count * col_width)
    values = gathered.astype(jnp.float32)
    factor = lax.rsqrt(jnp.mean(values * values, axis=-1, keepdims=True) + 1e-06)
    normed = (values * factor * norm_gain.astype(jnp.float32)).astype(jnp.bfloat16)
    width = normed.shape[1]
    shared_lin = jnp.dot(normed, shared_gate, preferred_element_type=jnp.float32)
    shared_pre = jnp.dot(normed, shared_up, preferred_element_type=jnp.float32)
    shared_act = (jax.nn.silu(shared_lin) * shared_pre).astype(jnp.bfloat16)

    request_end = jnp.cumsum(lengths)
    positions = dp_index * tok_rows + jnp.arange(tok_rows, dtype=jnp.int32)
    request_of = jnp.sum((request_end[None, :] <= positions[:, None]).astype(jnp.int32), axis=1)
    request_hot = (
        request_of[:, None] == jnp.arange(lengths.shape[0], dtype=jnp.int32)[None, :]
    ).astype(jnp.int32)
    slot_of = jnp.sum(request_hot * request_adapter[None, :], axis=1)
    chosen = (slot_of[:, None] == jnp.arange(active_count, dtype=jnp.int32)[None, :]).astype(
        jnp.float32
    )
    in_matrix = jnp.transpose(picked_in, (1, 0, 2)).reshape(
        shared_act.shape[1], active_count * rank_width
    )
    lowrank = jnp.dot(shared_act, in_matrix, preferred_element_type=jnp.float32)
    lowrank_sel = jnp.sum(
        lowrank.reshape(tok_rows, active_count, rank_width) * chosen[:, :, None], axis=1
    )
    lowrank_sel = lax.psum(lowrank_sel, "mp")
    lowrank = (chosen[:, :, None] * lowrank_sel[:, None, :]).reshape(
        tok_rows, active_count * rank_width
    )
    adapted = jnp.dot(
        lowrank,
        picked_out.reshape(active_count * rank_width, col_width).astype(jnp.float32),
        precision=lax.Precision.HIGHEST,
    )

    flat_routes = routes.reshape(-1)
    expert_hot = (
        flat_routes[:, None] == jnp.arange(total_experts, dtype=jnp.int32)[None, :]
    ).astype(jnp.int32)
    earlier = jnp.cumsum(expert_hot, axis=0) - expert_hot
    position = jnp.sum(earlier * expert_hot, axis=1)
    slot_index = (flat_routes * capacity + position).reshape(tok_rows, top_count)
    slot_count = total_experts * capacity
    slot_hit = slot_index[:, :, None] == jnp.arange(slot_count, dtype=jnp.int32)[None, None, :]
    dispatch = jnp.any(slot_hit, axis=1).astype(jnp.bfloat16)
    send_rows = jnp.einsum(
        "ts,td->sd", dispatch, normed, preferred_element_type=jnp.float32
    ).astype(jnp.bfloat16)
    send_rows = send_rows.reshape(dp_count, local_experts, capacity, width)
    rows_out = experts_kernel(
        lax.all_to_all(send_rows, "dp", split_axis=0, concat_axis=0, tiled=True),
        expert_gate,
        expert_up,
        expert_down,
        mp_count,
    )
    rows_out = rows_out.reshape(dp_count * mp_count, local_experts * capacity, col_width)
    returned = lax.all_to_all(rows_out, ("dp", "mp"), split_axis=0, concat_axis=0, tiled=True)
    returned = returned.reshape(dp_count, mp_count, local_experts * capacity, col_width)
    returned = jnp.sum(returned.astype(jnp.float32), axis=1).reshape(slot_count, col_width)
    combine = jnp.sum(
        jnp.where(slot_hit, route_weights[:, :, None], 0.0), axis=1
    )
    routed = jnp.dot(combine, returned, precision=lax.Precision.HIGHEST)

    shared_part = jnp.dot(shared_act, shared_down, preferred_element_type=jnp.float32)
    shared_part = shared_part.astype(jnp.bfloat16).reshape(tok_rows, mp_count, col_width)
    shared_part = lax.all_to_all(
        jnp.transpose(shared_part, (1, 0, 2)), "mp", split_axis=0, concat_axis=0, tiled=True
    )
    shared_part = jnp.sum(shared_part.astype(jnp.float32), axis=0)
    return (shared_part + adapted + routed).astype(jnp.bfloat16)


def solution(mesh):
    in_specs = (
        P("dp", "mp"),
        P(),
        P(None, "mp"),
        P(None, "mp"),
        P("mp", None),
        P("dp", None, "mp"),
        P("dp", None, "mp"),
        P("dp", "mp", None),
        P("dp", "mp", None),
        P("dp", None, None),
        P(),
        P(),
        P(),
        P("dp", None),
        P("dp", None),
    )
    out_specs = P("dp", "mp")

    return jax.shard_map(body, mesh=mesh, in_specs=in_specs, out_specs=out_specs, check_vma=False)
```

```python
import jax
import jax.numpy as jnp
from jax import lax
from jax.experimental import pallas as pl
from jax.experimental.pallas import tpu as pltpu
from jax.sharding import PartitionSpec as P


def _expert_kernel(x_ref, wg_ref, wu_ref, wd_ref, o_ref, inner_ref):
    @pl.when(pl.program_id(1) == 0)
    def _():
        x = x_ref[...]
        x = x.reshape(x.shape[0] * x.shape[1], x.shape[2])
        g = jnp.dot(x, wg_ref[...], preferred_element_type=jnp.float32)
        u = jnp.dot(x, wu_ref[...], preferred_element_type=jnp.float32)
        inner_ref[...] = (g / (1.0 + jnp.exp(-g)) * u).astype(inner_ref.dtype)

    out = jnp.dot(inner_ref[...], wd_ref[...], preferred_element_type=jnp.float32)
    o_ref[...] = out.astype(o_ref.dtype).reshape(o_ref.shape)


def experts_kernel(rows_in, expert_gate, expert_up, expert_down, parts):
    sources, local_experts, capacity, width = rows_in.shape
    hidden = expert_gate.shape[2]
    col_width = width // parts
    rows = sources * capacity
    flops = local_experts * 6 * rows * width * hidden
    nbytes = 2 * (2 * rows_in.size + expert_gate.size + expert_up.size + expert_down.size)
    return pl.pallas_call(
        _expert_kernel,
        grid=(local_experts, parts),
        in_specs=[
            pl.BlockSpec((sources, None, capacity, width), lambda j, m: (0, j, 0, 0)),
            pl.BlockSpec((None, width, hidden), lambda j, m: (j, 0, 0)),
            pl.BlockSpec((None, width, hidden), lambda j, m: (j, 0, 0)),
            pl.BlockSpec((None, hidden, col_width), lambda j, m: (j, 0, m)),
        ],
        out_specs=pl.BlockSpec(
            (sources, None, None, capacity, col_width), lambda j, m: (0, m, j, 0, 0)
        ),
        out_shape=jax.ShapeDtypeStruct(
            (sources, parts, local_experts, capacity, col_width), jnp.bfloat16
        ),
        scratch_shapes=[pltpu.VMEM((rows, hidden), jnp.bfloat16)],
        compiler_params=pltpu.CompilerParams(dimension_semantics=("arbitrary", "arbitrary")),
        cost_estimate=pl.CostEstimate(
            flops=flops, transcendentals=local_experts * rows * hidden, bytes_accessed=nbytes
        ),
    )(rows_in, expert_gate, expert_up, expert_down)


def mp_gather(x, mp_index, mp_count):
    shifted = [x] + [
        lax.ppermute(x, "mp", [(i, (i + k) % mp_count) for i in range(mp_count)])
        for k in range(1, mp_count)
    ]
    order = (mp_index - jnp.arange(mp_count, dtype=jnp.int32)) % mp_count
    blocks = jnp.moveaxis(jnp.take(jnp.stack(shifted), order, axis=0), 0, 1)
    return blocks.reshape(x.shape[0], mp_count * x.shape[1], *x.shape[2:])


def body(
    hidden,
    norm_gain,
    shared_gate,
    shared_up,
    shared_down,
    expert_gate,
    expert_up,
    expert_down,
    adapter_in,
    adapter_out,
    active,
    lengths,
    request_adapter,
    routes,
    route_weights,
):
    tok_rows = routes.shape[0]
    top_count = routes.shape[1]
    dp_count = lax.axis_size("dp")
    mp_count = lax.axis_size("mp")
    dp_index = lax.axis_index("dp")
    mp_index = lax.axis_index("mp")
    col_width = hidden.shape[1]
    local_experts = expert_gate.shape[0]
    total_experts = local_experts * dp_count
    capacity = mp_count * max(1, tok_rows * top_count * 4 // (total_experts * mp_count * 3))

    active_count = active.shape[0]
    rank_width = adapter_in.shape[2]
    local_adapters = adapter_in.shape[0]
    owned_ids = dp_index * local_adapters + jnp.arange(local_adapters, dtype=jnp.int32)
    selector = (active[:, None] == owned_ids[None, :]).astype(jnp.bfloat16)
    picked_in = jnp.einsum(
        "ji,isr->jsr", selector, mp_gather(adapter_in, mp_index, mp_count), preferred_element_type=jnp.float32
    ).astype(jnp.bfloat16)
    out_cols = lax.dynamic_slice_in_dim(adapter_out, mp_index * col_width, col_width, axis=2)
    picked_out = jnp.einsum(
        "ji,ird->jrd", selector, out_cols, preferred_element_type=jnp.float32
    ).astype(jnp.bfloat16)
    picked_in, picked_out = lax.psum((picked_in, picked_out), "dp")

    gathered = mp_gather(hidden, mp_index, mp_count)
    values = gathered.astype(jnp.float32)
    factor = lax.rsqrt(jnp.mean(values * values, axis=-1, keepdims=True) + 1e-06)
    normed = (values * factor * norm_gain.astype(jnp.float32)).astype(jnp.bfloat16)
    width = normed.shape[1]
    shared_lin = jnp.dot(normed, shared_gate, preferred_element_type=jnp.float32)
    shared_pre = jnp.dot(normed, shared_up, preferred_element_type=jnp.float32)
    shared_act = (jax.nn.silu(shared_lin) * shared_pre).astype(jnp.bfloat16)

    request_end = jnp.cumsum(lengths)
    positions = dp_index * tok_rows + jnp.arange(tok_rows, dtype=jnp.int32)
    request_of = jnp.sum((request_end[None, :] <= positions[:, None]).astype(jnp.int32), axis=1)
    request_hot = (
        request_of[:, None] == jnp.arange(lengths.shape[0], dtype=jnp.int32)[None, :]
    ).astype(jnp.int32)
    slot_of = jnp.sum(request_hot * request_adapter[None, :], axis=1)
    chosen = (slot_of[:, None] == jnp.arange(active_count, dtype=jnp.int32)[None, :]).astype(
        jnp.float32
    )
    shared_full = mp_gather(shared_act, mp_index, mp_count)
    in_matrix = jnp.transpose(picked_in, (1, 0, 2)).reshape(
        shared_full.shape[1], active_count * rank_width
    )
    lowrank = jnp.dot(shared_full, in_matrix, preferred_element_type=jnp.float32)
    lowrank = (lowrank.reshape(tok_rows, active_count, rank_width) * chosen[:, :, None]).reshape(
        tok_rows, active_count * rank_width
    )
    adapted = jnp.dot(
        lowrank,
        picked_out.reshape(active_count * rank_width, col_width).astype(jnp.float32),
        precision=lax.Precision.HIGHEST,
    )

    flat_routes = routes.reshape(-1)
    expert_hot = (
        flat_routes[:, None] == jnp.arange(total_experts, dtype=jnp.int32)[None, :]
    ).astype(jnp.int32)
    earlier = jnp.cumsum(expert_hot, axis=0) - expert_hot
    position = jnp.sum(earlier * expert_hot, axis=1)
    slot_index = (flat_routes * capacity + position).reshape(tok_rows, top_count)
    slot_count = total_experts * capacity
    slot_hit = slot_index[:, :, None] == jnp.arange(slot_count, dtype=jnp.int32)[None, None, :]
    dispatch = jnp.any(slot_hit, axis=1).astype(jnp.bfloat16)
    send_rows = jnp.einsum(
        "ts,td->sd", dispatch, normed, preferred_element_type=jnp.float32
    ).astype(jnp.bfloat16)
    send_rows = send_rows.reshape(dp_count, local_experts, capacity, width)
    rows_out = experts_kernel(
        lax.all_to_all(send_rows, "dp", split_axis=0, concat_axis=0, tiled=True),
        expert_gate,
        expert_up,
        expert_down,
        mp_count,
    )
    rows_out = rows_out.reshape(dp_count * mp_count, local_experts * capacity, col_width)
    returned = lax.all_to_all(rows_out, ("dp", "mp"), split_axis=0, concat_axis=0, tiled=True)
    returned = returned.reshape(dp_count, mp_count, local_experts * capacity, col_width)
    returned = jnp.sum(returned.astype(jnp.float32), axis=1).reshape(slot_count, col_width)
    combine = jnp.sum(
        jnp.where(slot_hit, route_weights[:, :, None], 0.0), axis=1
    )
    routed = jnp.dot(combine, returned, precision=lax.Precision.HIGHEST)

    shared_part = jnp.dot(shared_act, shared_down, preferred_element_type=jnp.float32)
    shared_part = shared_part.astype(jnp.bfloat16)
    shared_sum = lax.dynamic_slice_in_dim(
        shared_part, mp_index * col_width, col_width, axis=1
    ).astype(jnp.float32)
    for k in range(1, mp_count):
        target = (mp_index + k) % mp_count
        piece = lax.dynamic_slice_in_dim(shared_part, target * col_width, col_width, axis=1)
        piece = lax.ppermute(piece, "mp", [(i, (i + k) % mp_count) for i in range(mp_count)])
        shared_sum = shared_sum + piece.astype(jnp.float32)
    shared_part = shared_sum
    return (shared_part + adapted + routed).astype(jnp.bfloat16)


def solution(mesh):
    in_specs = (
        P("dp", "mp"),
        P(),
        P(None, "mp"),
        P(None, "mp"),
        P("mp", None),
        P("dp", None, "mp"),
        P("dp", None, "mp"),
        P("dp", "mp", None),
        P("dp", "mp", None),
        P("dp", None, None),
        P(),
        P(),
        P(),
        P("dp", None),
        P("dp", None),
    )
    out_specs = P("dp", "mp")

    return jax.shard_map(body, mesh=mesh, in_specs=in_specs, out_specs=out_specs, check_vma=False)
```

```python
import jax
import jax.numpy as jnp
from jax import lax
from jax.experimental import pallas as pl
from jax.experimental.pallas import tpu as pltpu
from jax.sharding import PartitionSpec as P


def _expert_kernel(x_ref, wg_ref, wu_ref, wd_ref, o_ref, inner_ref):
    chunks = 4
    step = x_ref.shape[0] // chunks
    rows = step * x_ref.shape[1]

    @pl.when(pl.program_id(1) == 0)
    def _():
        for r in range(chunks):
            x = x_ref[r * step:(r + 1) * step].reshape(rows, x_ref.shape[2])
            g = jnp.dot(x, wg_ref[...], preferred_element_type=jnp.float32)
            u = jnp.dot(x, wu_ref[...], preferred_element_type=jnp.float32)
            inner_ref[r * rows:(r + 1) * rows] = (g / (1.0 + jnp.exp(-g)) * u).astype(
                inner_ref.dtype
            )

    for r in range(chunks):
        out = jnp.dot(
            inner_ref[r * rows:(r + 1) * rows], wd_ref[...], preferred_element_type=jnp.float32
        )
        o_ref[r * step:(r + 1) * step] = out.astype(o_ref.dtype).reshape(
            step, o_ref.shape[1], o_ref.shape[2]
        )


def experts_kernel(rows_in, expert_gate, expert_up, expert_down, parts):
    sources, local_experts, capacity, width = rows_in.shape
    hidden = expert_gate.shape[2]
    col_width = width // parts
    rows = sources * capacity
    flops = local_experts * 6 * rows * width * hidden
    nbytes = 2 * (2 * rows_in.size + expert_gate.size + expert_up.size + expert_down.size)
    return pl.pallas_call(
        _expert_kernel,
        grid=(local_experts, parts),
        in_specs=[
            pl.BlockSpec((sources, None, capacity, width), lambda j, m: (0, j, 0, 0)),
            pl.BlockSpec((None, width, hidden), lambda j, m: (j, 0, 0)),
            pl.BlockSpec((None, width, hidden), lambda j, m: (j, 0, 0)),
            pl.BlockSpec((None, hidden, col_width), lambda j, m: (j, 0, m)),
        ],
        out_specs=pl.BlockSpec(
            (sources, None, None, capacity, col_width), lambda j, m: (0, m, j, 0, 0)
        ),
        out_shape=jax.ShapeDtypeStruct(
            (sources, parts, local_experts, capacity, col_width), jnp.bfloat16
        ),
        scratch_shapes=[pltpu.VMEM((rows, hidden), jnp.bfloat16)],
        compiler_params=pltpu.CompilerParams(dimension_semantics=("arbitrary", "arbitrary")),
        cost_estimate=pl.CostEstimate(
            flops=flops, transcendentals=local_experts * rows * hidden, bytes_accessed=nbytes
        ),
    )(rows_in, expert_gate, expert_up, expert_down)


def body(
    hidden,
    norm_gain,
    shared_gate,
    shared_up,
    shared_down,
    expert_gate,
    expert_up,
    expert_down,
    adapter_in,
    adapter_out,
    active,
    lengths,
    request_adapter,
    routes,
    route_weights,
):
    tok_rows = routes.shape[0]
    top_count = routes.shape[1]
    dp_count = lax.axis_size("dp")
    mp_count = lax.axis_size("mp")
    dp_index = lax.axis_index("dp")
    mp_index = lax.axis_index("mp")
    col_width = hidden.shape[1]
    local_experts = expert_gate.shape[0]
    total_experts = local_experts * dp_count
    capacity = mp_count * max(1, tok_rows * top_count * 4 // (total_experts * mp_count * 3))

    active_count = active.shape[0]
    rank_width = adapter_in.shape[2]
    local_adapters = adapter_in.shape[0]
    owned_ids = dp_index * local_adapters + jnp.arange(local_adapters, dtype=jnp.int32)
    selector = (active[:, None] == owned_ids[None, :]).astype(jnp.bfloat16)
    picked_in = jnp.einsum(
        "ji,isr->jsr", selector, adapter_in, preferred_element_type=jnp.float32
    ).astype(jnp.bfloat16)
    out_cols = lax.dynamic_slice_in_dim(adapter_out, mp_index * col_width, col_width, axis=2)
    picked_out = jnp.einsum(
        "ji,ird->jrd", selector, out_cols, preferred_element_type=jnp.float32
    ).astype(jnp.bfloat16)
    picked_in, picked_out = lax.psum((picked_in, picked_out), "dp")

    shifted = [hidden] + [
        lax.ppermute(hidden, "mp", [(i, (i + k) % mp_count) for i in range(mp_count)])
        for k in range(1, mp_count)
    ]
    order = (mp_index - jnp.arange(mp_count, dtype=jnp.int32)) % mp_count
    blocks = jnp.take(jnp.stack(shifted), order, axis=0)
    gathered = jnp.transpose(blocks, (1, 0, 2)).reshape(tok_rows, mp_count * col_width)
    values = gathered.astype(jnp.float32)
    factor = lax.rsqrt(jnp.mean(values * values, axis=-1, keepdims=True) + 1e-06)
    normed = (values * factor * norm_gain.astype(jnp.float32)).astype(jnp.bfloat16)
    width = normed.shape[1]
    shared_lin = jnp.dot(normed, shared_gate, preferred_element_type=jnp.float32)
    shared_pre = jnp.dot(normed, shared_up, preferred_element_type=jnp.float32)
    shared_act = (jax.nn.silu(shared_lin) * shared_pre).astype(jnp.bfloat16)

    request_end = jnp.cumsum(lengths)
    positions = dp_index * tok_rows + jnp.arange(tok_rows, dtype=jnp.int32)
    request_of = jnp.sum((request_end[None, :] <= positions[:, None]).astype(jnp.int32), axis=1)
    request_hot = (
        request_of[:, None] == jnp.arange(lengths.shape[0], dtype=jnp.int32)[None, :]
    ).astype(jnp.int32)
    slot_of = jnp.sum(request_hot * request_adapter[None, :], axis=1)
    chosen = (slot_of[:, None] == jnp.arange(active_count, dtype=jnp.int32)[None, :]).astype(
        jnp.float32
    )
    in_matrix = jnp.transpose(picked_in, (1, 0, 2)).reshape(
        shared_act.shape[1], active_count * rank_width
    )
    lowrank = jnp.dot(shared_act, in_matrix, preferred_element_type=jnp.float32)
    lowrank_sel = jnp.sum(
        lowrank.reshape(tok_rows, active_count, rank_width) * chosen[:, :, None], axis=1
    )
    lowrank_sel = lax.psum(lowrank_sel, "mp")
    lowrank = (chosen[:, :, None] * lowrank_sel[:, None, :]).reshape(
        tok_rows, active_count * rank_width
    )
    adapted = jnp.dot(
        lowrank,
        picked_out.reshape(active_count * rank_width, col_width).astype(jnp.float32),
        precision=lax.Precision.HIGHEST,
    )

    flat_routes = routes.reshape(-1)
    expert_hot = (
        flat_routes[:, None] == jnp.arange(total_experts, dtype=jnp.int32)[None, :]
    ).astype(jnp.int32)
    earlier = jnp.cumsum(expert_hot, axis=0) - expert_hot
    position = jnp.sum(earlier * expert_hot, axis=1)
    slot_index = (flat_routes * capacity + position).reshape(tok_rows, top_count)
    slot_count = total_experts * capacity
    slot_hit = slot_index[:, :, None] == jnp.arange(slot_count, dtype=jnp.int32)[None, None, :]
    dispatch = jnp.any(slot_hit, axis=1).astype(jnp.bfloat16)
    send_rows = jnp.einsum(
        "ts,td->sd", dispatch, normed, preferred_element_type=jnp.float32
    ).astype(jnp.bfloat16)
    send_rows = send_rows.reshape(dp_count, local_experts, capacity, width)
    rows_out = experts_kernel(
        lax.all_to_all(send_rows, "dp", split_axis=0, concat_axis=0, tiled=True),
        expert_gate,
        expert_up,
        expert_down,
        mp_count,
    )
    rows_out = rows_out.reshape(dp_count * mp_count, local_experts * capacity, col_width)
    returned = lax.all_to_all(rows_out, ("dp", "mp"), split_axis=0, concat_axis=0, tiled=True)
    returned = returned.reshape(dp_count, mp_count, local_experts * capacity, col_width)
    returned = jnp.sum(returned.astype(jnp.float32), axis=1).reshape(slot_count, col_width)
    combine = jnp.sum(
        jnp.where(slot_hit, route_weights[:, :, None], 0.0), axis=1
    )
    routed = jnp.dot(combine, returned, precision=lax.Precision.HIGHEST)

    shared_part = jnp.dot(shared_act, shared_down, preferred_element_type=jnp.float32)
    shared_part = shared_part.astype(jnp.bfloat16)
    shared_sum = lax.dynamic_slice_in_dim(
        shared_part, mp_index * col_width, col_width, axis=1
    ).astype(jnp.float32)
    for k in range(1, mp_count):
        target = (mp_index + k) % mp_count
        piece = lax.dynamic_slice_in_dim(shared_part, target * col_width, col_width, axis=1)
        piece = lax.ppermute(piece, "mp", [(i, (i + k) % mp_count) for i in range(mp_count)])
        shared_sum = shared_sum + piece.astype(jnp.float32)
    shared_part = shared_sum
    return (shared_part + adapted + routed).astype(jnp.bfloat16)


def solution(mesh):
    in_specs = (
        P("dp", "mp"),
        P(),
        P(None, "mp"),
        P(None, "mp"),
        P("mp", None),
        P("dp", None, "mp"),
        P("dp", None, "mp"),
        P("dp", "mp", None),
        P("dp", "mp", None),
        P("dp", None, None),
        P(),
        P(),
        P(),
        P("dp", None),
        P("dp", None),
    )
    out_specs = P("dp", "mp")

    return jax.shard_map(body, mesh=mesh, in_specs=in_specs, out_specs=out_specs, check_vma=False)
```

```python
import jax
import jax.numpy as jnp
from jax import lax
from jax.experimental import pallas as pl
from jax.experimental.pallas import tpu as pltpu
from jax.sharding import PartitionSpec as P


def _expert_kernel(x_ref, wg_ref, wu_ref, wd_ref, o_ref, inner_ref):
    @pl.when(pl.program_id(1) == 0)
    def _():
        x = x_ref[...]
        x = x.reshape(x.shape[0] * x.shape[1], x.shape[2])
        g = jnp.dot(x, wg_ref[...], preferred_element_type=jnp.float32)
        u = jnp.dot(x, wu_ref[...], preferred_element_type=jnp.float32)
        inner_ref[...] = (g / (1.0 + jnp.exp(-g)) * u).astype(inner_ref.dtype)

    out = jnp.dot(inner_ref[...], wd_ref[...], preferred_element_type=jnp.float32)
    o_ref[...] = out.astype(o_ref.dtype).reshape(o_ref.shape)


def experts_kernel(rows_in, expert_gate, expert_up, expert_down, parts):
    sources, local_experts, capacity, width = rows_in.shape
    hidden = expert_gate.shape[2]
    col_width = width // parts
    rows = sources * capacity
    flops = local_experts * 6 * rows * width * hidden
    nbytes = 2 * (2 * rows_in.size + expert_gate.size + expert_up.size + expert_down.size)
    return pl.pallas_call(
        _expert_kernel,
        grid=(local_experts, parts),
        in_specs=[
            pl.BlockSpec((sources, None, capacity, width), lambda j, m: (0, j, 0, 0)),
            pl.BlockSpec((None, width, hidden), lambda j, m: (j, 0, 0)),
            pl.BlockSpec((None, width, hidden), lambda j, m: (j, 0, 0)),
            pl.BlockSpec((None, hidden, col_width), lambda j, m: (j, 0, m)),
        ],
        out_specs=pl.BlockSpec(
            (sources, None, None, capacity, col_width), lambda j, m: (0, m, j, 0, 0)
        ),
        out_shape=jax.ShapeDtypeStruct(
            (sources, parts, local_experts, capacity, col_width), jnp.bfloat16
        ),
        scratch_shapes=[pltpu.VMEM((rows, hidden), jnp.bfloat16)],
        compiler_params=pltpu.CompilerParams(dimension_semantics=("arbitrary", "arbitrary")),
        cost_estimate=pl.CostEstimate(
            flops=flops, transcendentals=local_experts * rows * hidden, bytes_accessed=nbytes
        ),
    )(rows_in, expert_gate, expert_up, expert_down)


def body(
    hidden,
    norm_gain,
    shared_gate,
    shared_up,
    shared_down,
    expert_gate,
    expert_up,
    expert_down,
    adapter_in,
    adapter_out,
    active,
    lengths,
    request_adapter,
    routes,
    route_weights,
):
    tok_rows = routes.shape[0]
    top_count = routes.shape[1]
    dp_count = lax.axis_size("dp")
    mp_count = lax.axis_size("mp")
    dp_index = lax.axis_index("dp")
    mp_index = lax.axis_index("mp")
    col_width = hidden.shape[1]
    local_experts = expert_gate.shape[0]
    total_experts = local_experts * dp_count
    capacity = mp_count * max(1, tok_rows * top_count * 4 // (total_experts * mp_count * 3))

    active_count = active.shape[0]
    rank_width = adapter_in.shape[2]
    local_adapters = adapter_in.shape[0]
    owned_ids = dp_index * local_adapters + jnp.arange(local_adapters, dtype=jnp.int32)
    selector = (active[:, None] == owned_ids[None, :]).astype(jnp.bfloat16)
    picked_in = jnp.einsum(
        "ji,isr->jsr", selector, adapter_in, preferred_element_type=jnp.float32
    ).astype(jnp.bfloat16)
    out_cols = lax.dynamic_slice_in_dim(adapter_out, mp_index * col_width, col_width, axis=2)
    picked_out = jnp.einsum(
        "ji,ird->jrd", selector, out_cols, preferred_element_type=jnp.float32
    ).astype(jnp.bfloat16)
    picked_in, picked_out = lax.psum((picked_in, picked_out), "dp")

    shifted = [hidden] + [
        lax.ppermute(hidden, "mp", [(i, (i + k) % mp_count) for i in range(mp_count)])
        for k in range(1, mp_count)
    ]
    order = (mp_index - jnp.arange(mp_count, dtype=jnp.int32)) % mp_count
    blocks = jnp.take(jnp.stack(shifted), order, axis=0)
    gathered = jnp.transpose(blocks, (1, 0, 2)).reshape(tok_rows, mp_count * col_width)
    values = gathered.astype(jnp.float32)
    factor = lax.rsqrt(jnp.mean(values * values, axis=-1, keepdims=True) + 1e-06)
    normed = (values * factor * norm_gain.astype(jnp.float32)).astype(jnp.bfloat16)
    width = normed.shape[1]
    shared_lin = jnp.dot(normed, shared_gate, preferred_element_type=jnp.float32)
    shared_pre = jnp.dot(normed, shared_up, preferred_element_type=jnp.float32)
    shared_act = (jax.nn.silu(shared_lin) * shared_pre).astype(jnp.bfloat16)

    request_end = jnp.cumsum(lengths)
    positions = dp_index * tok_rows + jnp.arange(tok_rows, dtype=jnp.int32)
    request_of = jnp.sum((request_end[None, :] <= positions[:, None]).astype(jnp.int32), axis=1)
    request_hot = (
        request_of[:, None] == jnp.arange(lengths.shape[0], dtype=jnp.int32)[None, :]
    ).astype(jnp.int32)
    slot_of = jnp.sum(request_hot * request_adapter[None, :], axis=1)
    chosen = (slot_of[:, None] == jnp.arange(active_count, dtype=jnp.int32)[None, :]).astype(
        jnp.float32
    )
    in_matrix = jnp.transpose(picked_in, (1, 0, 2)).reshape(
        shared_act.shape[1], active_count * rank_width
    )
    lowrank = jnp.dot(shared_act, in_matrix, preferred_element_type=jnp.float32)
    lowrank_sel = jnp.sum(
        lowrank.reshape(tok_rows, active_count, rank_width) * chosen[:, :, None], axis=1
    )
    lowrank_sel = lax.psum(lowrank_sel, "mp")
    lowrank = (chosen[:, :, None] * lowrank_sel[:, None, :]).reshape(
        tok_rows, active_count * rank_width
    )
    adapted = jnp.dot(
        lowrank,
        picked_out.reshape(active_count * rank_width, col_width).astype(jnp.float32),
        precision=lax.Precision.HIGH,
    )

    flat_routes = routes.reshape(-1)
    expert_hot = (
        flat_routes[:, None] == jnp.arange(total_experts, dtype=jnp.int32)[None, :]
    ).astype(jnp.int32)
    earlier = jnp.cumsum(expert_hot, axis=0) - expert_hot
    position = jnp.sum(earlier * expert_hot, axis=1)
    slot_index = (flat_routes * capacity + position).reshape(tok_rows, top_count)
    slot_count = total_experts * capacity
    slot_hit = slot_index[:, :, None] == jnp.arange(slot_count, dtype=jnp.int32)[None, None, :]
    dispatch = jnp.any(slot_hit, axis=1).astype(jnp.bfloat16)
    send_rows = jnp.einsum(
        "ts,td->sd", dispatch, normed, preferred_element_type=jnp.float32
    ).astype(jnp.bfloat16)
    send_rows = send_rows.reshape(dp_count, local_experts, capacity, width)
    rows_out = experts_kernel(
        lax.all_to_all(send_rows, "dp", split_axis=0, concat_axis=0, tiled=True),
        expert_gate,
        expert_up,
        expert_down,
        mp_count,
    )
    rows_out = rows_out.reshape(dp_count * mp_count, local_experts * capacity, col_width)
    returned = lax.all_to_all(rows_out, ("dp", "mp"), split_axis=0, concat_axis=0, tiled=True)
    returned = returned.reshape(dp_count, mp_count, local_experts * capacity, col_width)
    returned = jnp.sum(returned.astype(jnp.float32), axis=1).reshape(slot_count, col_width)
    combine = jnp.sum(
        jnp.where(slot_hit, route_weights[:, :, None], 0.0), axis=1
    )
    routed = jnp.dot(combine, returned, precision=lax.Precision.HIGH)

    shared_part = jnp.dot(shared_act, shared_down, preferred_element_type=jnp.float32)
    shared_part = shared_part.astype(jnp.bfloat16)
    shared_sum = lax.dynamic_slice_in_dim(
        shared_part, mp_index * col_width, col_width, axis=1
    ).astype(jnp.float32)
    for k in range(1, mp_count):
        target = (mp_index + k) % mp_count
        piece = lax.dynamic_slice_in_dim(shared_part, target * col_width, col_width, axis=1)
        piece = lax.ppermute(piece, "mp", [(i, (i + k) % mp_count) for i in range(mp_count)])
        shared_sum = shared_sum + piece.astype(jnp.float32)
    shared_part = shared_sum
    return (shared_part + adapted + routed).astype(jnp.bfloat16)


def solution(mesh):
    in_specs = (
        P("dp", "mp"),
        P(),
        P(None, "mp"),
        P(None, "mp"),
        P("mp", None),
        P("dp", None, "mp"),
        P("dp", None, "mp"),
        P("dp", "mp", None),
        P("dp", "mp", None),
        P("dp", None, None),
        P(),
        P(),
        P(),
        P("dp", None),
        P("dp", None),
    )
    out_specs = P("dp", "mp")

    return jax.shard_map(body, mesh=mesh, in_specs=in_specs, out_specs=out_specs, check_vma=False)
```
